256 devices in a mesh: heads: 4 (over y), seq: 64 (over z, x, core).
Axes of the slice: x: 4, y: 4, z: 8, core: 2. Of those that a mesh axis runs over, the one named last changes fastest.
Arguments:
- hidden: bfloat16 [64, 2048], P(None, 'seq')
- w_qkv: bfloat16 [2048, 3, 2048], P('seq', None, 'heads')
- w_out: bfloat16 [2048, 2048], P('heads', 'seq'), may hold values from -0.125 to 0.125
- positions: int32 [64], replicated, may hold values from 0 to 8191
- req_blocks: int32 [64], replicated, may hold values from 1 to 64, 1152 in all
- keep_list: int32 [1152], P('seq'), may hold values from 0 to 1, as said below
- dest_slot: int32 [1152], P('seq'), may hold values from 0 to 1023, as said below
- key_cache: bfloat16 [1152, 128, 2048], P('seq', None, 'heads')
- value_cache: bfloat16 [1152, 128, 2048], P('seq', None, 'heads')
- fold_weight: float32 [1152, 128], P('seq'), may hold values from 0.1 to 10
Outputs:
- packed_keys: bfloat16 [1024, 128, 2048], P('seq', None, 'heads')
- packed_values: bfloat16 [1024, 128, 2048], P('seq', None, 'heads')
- packed_request: int32 [1024], P('seq')
- folded_keys: bfloat16 [1152, 2048], P('seq', 'heads')
- folded_values: bfloat16 [1152, 2048], P('seq', 'heads')
- attn_out: bfloat16 [64, 2048], P(None, 'seq')
The draws below stay inside these ranges and needn't reach their ends.
Inputs may be any that keep to these rules, and one draw needn't show every extreme that they name: `keep_list`: each index of seq (its 18 blocks) keeps at most 15 blocks, and some index keeps exactly that many. `dest_slot`: for a kept block: its slot among 1024 packed slots, 16 to each owner (owner = slot // 16); kept blocks have distinct slots; a kept block held by index i of seq goes to owner (i + j) mod 64 for some j with 0 <= j < 4; at most 4 kept blocks of one index share an owner, and some index sends that many to one owner; some owner has all its slots filled. Entries of dropped blocks are meaningless.
All inputs are finite; a program needn't handle non-finite values.
Results may differ from the reference program's by a relative error of at most 0.0156.
The reference program's roundings to bfloat16 on the way count: a program that leaves them out, or rounds other values in their place, can miss the bound.
Values may be sent and summed in bfloat16 or wider, within the bound.
No kernel may reach another device: no remote copies, remote signals or barrier semaphores. Data moves between devices by JAX's collectives and lax.ppermute only.
A program may use at most 128 MiB of HBM per device.

```python
import math
import jax
import jax.numpy as jnp
import numpy as np
from jax import lax

D = 2048
HEADS = 32
HDIM = 64
ROWS = 128
HOPS = 4
REQS = 64
BLK_DEV = 18
KEEP_MOST = 15
CAP = 4
SLOT_DEV = 16
BLOCKS = 1152
SLOTS = 1024
MOST_BLK = 64
N_SEQ = 64


def plan_blocks(key):
    keys = jax.random.split(jax.random.fold_in(key, 7), 7)
    dev_count = N_SEQ
    block_count = BLK_DEV
    most = KEEP_MOST
    hop_count = HOPS
    cap_each = CAP
    device_ids = jnp.arange(dev_count)
    counts = jax.random.randint(keys[0], (dev_count,), most // 2, most + 1)
    rotation = jax.random.randint(keys[1], (dev_count,), 0, hop_count)
    full_owner = jax.random.randint(keys[2], (), 0, dev_count)
    feeders = (full_owner - jnp.arange(hop_count)) % dev_count
    rotation = rotation.at[feeders].set(jnp.arange(hop_count))
    counts = counts.at[feeders].max((cap_each - 1) * hop_count + 1)
    full_device = jax.random.randint(keys[3], (), 0, dev_count)
    counts = jnp.where(device_ids == full_device, most, counts)
    orders = jax.vmap(lambda sub: jax.random.permutation(sub, block_count))(jax.random.split(keys[4], dev_count))
    positions_in_order = jnp.argsort(orders, axis=1)
    keep_table = (positions_in_order < counts[:, None]).astype(jnp.int32)
    kept_rank = jnp.cumsum(keep_table, axis=1) - keep_table
    hop_table = (kept_rank + rotation[:, None]) % hop_count
    owners = (device_ids[:, None] + hop_table) % dev_count
    local_index = jnp.minimum(hop_table * cap_each + kept_rank // hop_count, SLOT_DEV - 1)
    slot_perms = jax.vmap(lambda sub: jax.random.permutation(sub, SLOT_DEV))(jax.random.split(keys[5], dev_count))
    local_slot = slot_perms[owners, local_index]
    slots = owners * SLOT_DEV + local_slot
    filler = jax.random.randint(keys[6], (dev_count, block_count), 0, SLOTS)
    dest_table = jnp.where(keep_table == 1, slots, filler)
    return (keep_table.reshape(-1).astype(jnp.int32), dest_table.reshape(-1).astype(jnp.int32))


def draw_keep_list(key, part):
    return plan_blocks(key)[0]


def draw_dest_slot(key, part):
    return plan_blocks(key)[1]


def draw_w_qkv(key, part):
    keys = jax.random.split(jax.random.fold_in(key, 11), 3)
    width = HEADS * HDIM
    factor = 1.0 / math.sqrt(D)
    query_part = jax.random.truncated_normal(keys[0], -3.0, 3.0, (D, width), jnp.float32) * factor
    key_part = query_part + 0.25 * jax.random.truncated_normal(keys[1], -3.0, 3.0, (D, width), jnp.float32) * factor
    value_part = jax.random.truncated_normal(keys[2], -3.0, 3.0, (D, width), jnp.float32) * factor
    return jnp.stack([query_part, key_part, value_part], axis=1).astype(jnp.bfloat16)


def draw_hidden(key, part):
    keys = jax.random.split(key, 3)
    col_scale = 10.0 ** (jnp.arange(D, dtype=jnp.float32) / D - 0.5) * jnp.exp(jax.random.uniform(keys[0], (D,), jnp.float32, -0.3, 0.3))
    row_scale = jnp.exp(jax.random.uniform(keys[1], (REQS, 1), jnp.float32, math.log(0.3), math.log(3.0)))
    base = jax.random.normal(keys[2], (REQS, D), jnp.float32)
    return (base * row_scale * col_scale[None, :]).astype(jnp.bfloat16)


def draw_key_cache(key, part):
    keys = jax.random.split(key, 1)
    shape = (BLOCKS, ROWS, HEADS * HDIM)
    base = jax.random.normal(keys[0], shape, jnp.float32)
    return base.astype(jnp.bfloat16)


def draw_value_cache(key, part):
    keys = jax.random.split(key, 2)
    shape = (BLOCKS, ROWS, HEADS * HDIM)
    offsets = jax.random.uniform(keys[0], (BLOCKS, 1, HEADS * HDIM), jnp.float32, -2.0, 2.0)
    noise = 0.5 * jax.random.normal(keys[1], shape, jnp.float32)
    return (offsets + noise).astype(jnp.bfloat16)


def touch_ends(array, key, smallest, high):
    extent = array.shape
    index_at = [jax.random.randint(jax.random.fold_in(key, axis), (), 0, extent[axis]) for axis in range(len(extent))]
    array = array.at[tuple(index_at)].set(smallest)
    longest = extent.index(max(extent))
    index_at[longest] = (index_at[longest] + 1) % extent[longest]
    return array.at[tuple(index_at)].set(high)


def block_scale(stream_key, shape, shards, smallest, high):
    def one(dim, shards_of):
        steps = jax.random.uniform(jax.random.fold_in(jax.random.fold_in(stream_key, 6), dim), (shards_of,), jnp.float32, smallest / len(shards), high / len(shards))
        return jnp.repeat(jnp.exp(steps), shape[dim] // shards_of).reshape((-1,) + (1,) * (len(shape) - dim - 1))

    factor_of = one(*shards[0])
    for cut in shards[1:]:
        factor_of = factor_of * one(*cut)
    return factor_of


def length_profile(amount, total, most, skew):
    loads = [(1 << 20) // math.isqrt(rank ** skew) + 1 for rank in range(2, amount + 1)]
    rest, holding = total - most - (amount - 1), [1] * (amount - 1)
    while rest > 0:
        movable = [i for i in range(amount - 1) if holding[i] < most]
        whole, budget = sum([loads[i] for i in movable]), rest
        for i in movable:
            extra = min(most - holding[i], max(1, budget * loads[i] // whole), rest)
            holding[i] = holding[i] + extra
            rest = rest - extra
    return np.array([most] + holding)


def uneven(stream_key, count, total, bound, lean):
    if count == 2:
        one = jax.random.randint(stream_key, (), max(1, total - bound), min(bound, total - 1) + 1)
        return jnp.stack([one, total - one])
    tallies = jnp.asarray(length_profile(count, total, bound, lean), jnp.int32)
    couples = (count - 1) // 2
    giver, receiver = tallies[1:1 + 2 * couples:2], tallies[2:2 + 2 * couples:2]
    room = jnp.minimum(giver - 1, bound - receiver)
    shifted = jax.random.randint(jax.random.fold_in(stream_key, 1), (couples,), 0, 1 << 20) % (room + 1)
    tallies = tallies.at[1:1 + 2 * couples:2].set(giver - shifted).at[2:2 + 2 * couples:2].set(receiver + shifted)
    return tallies[jax.random.permutation(jax.random.fold_in(stream_key, 2), count)]


def normal_values(own_key, dims, spread, most, cuts=(), kind=jnp.bfloat16):
    result = spread * jax.random.normal(own_key, dims, jnp.float32)
    if cuts:
        result = result * block_scale(own_key, dims, cuts, -0.22, 0.18)
    return jnp.clip(result, -most, most).astype(kind)


def setup_inputs(seed: int = 0) -> dict:
    seeds = jax.random.split(jax.random.key(seed), 11)
    return {
        "hidden": draw_hidden(jax.random.fold_in(seeds[10], 71), 0),
        "w_qkv": draw_w_qkv(jax.random.fold_in(seeds[10], 71), 0),
        "w_out": normal_values(seeds[2], (HEADS * HDIM, D), (HEADS * HDIM) ** -0.5, 0.125, ((0, 4), (1, 64))),
        "positions": touch_ends(jax.random.randint(seeds[3], (REQS,), 0, 8192), jax.random.fold_in(seeds[3], 1), 0, 8191).astype(jnp.int32),
        "req_blocks": uneven(seeds[4], REQS, BLOCKS, MOST_BLK, 2).astype(jnp.int32),
        "keep_list": draw_keep_list(jax.random.fold_in(seeds[10], 71), 0),
        "dest_slot": draw_dest_slot(jax.random.fold_in(seeds[10], 71), 0),
        "key_cache": draw_key_cache(jax.random.fold_in(seeds[10], 71), 0),
        "value_cache": draw_value_cache(jax.random.fold_in(seeds[10], 71), 0),
        "fold_weight": jnp.clip(jnp.exp(math.log(10.0) - 4.6051702 * jax.random.uniform(seeds[9], (BLOCKS, ROWS), jnp.float32) ** block_scale(seeds[9], (BLOCKS, ROWS), ((0, 64),), -0.2, 0.2)), 0.1, 10.0),
    }


ROPE_BASE = 130000.0
NORM_EPSILON = 1e-05

def rotate_half(values, cos_table, sin_table):
    half = values.shape[-1] // 2
    lower = values[..., :half]
    upper = values[..., half:]
    return jnp.concatenate([lower * cos_table - upper * sin_table, upper * cos_table + lower * sin_table], axis=-1)

def rope_tables(positions, head_size):
    half = head_size // 2
    freqs = ROPE_BASE ** (-(2.0 * jnp.arange(half, dtype=jnp.float32)) / head_size)
    angles = positions.astype(jnp.float32)[:, None] * freqs[None, :]
    return (jnp.cos(angles)[:, None, :], jnp.sin(angles)[:, None, :])

def fold_block(inputs):
    weights, keys_block, values_block = inputs
    weight_sum = jnp.sum(weights)
    fold_keys = jnp.dot(weights, keys_block.astype(jnp.float32), precision=lax.Precision.HIGHEST) / weight_sum
    fold_values = jnp.dot(weights, values_block.astype(jnp.float32), precision=lax.Precision.HIGHEST) / weight_sum
    return (fold_keys, fold_values)

def reference(hidden, w_qkv, w_out, positions, req_blocks, keep_list, dest_slot, key_cache, value_cache, fold_weight):
    width = HEADS * HDIM
    widened = hidden.astype(jnp.float32)
    mean_square = lax.optimization_barrier(jnp.mean(widened * widened, axis=1, keepdims=True))
    normed = (widened * lax.rsqrt(mean_square + NORM_EPSILON)).astype(jnp.bfloat16)
    proj_all = jnp.dot(normed, w_qkv.reshape(D, 3 * width), preferred_element_type=jnp.float32)
    proj_all = proj_all.reshape(REQS, 3, HEADS, HDIM)
    cos_table, sin_table = rope_tables(positions, HDIM)
    queries = rotate_half(proj_all[:, 0], cos_table, sin_table).astype(jnp.bfloat16)
    new_keys = rotate_half(proj_all[:, 1], cos_table, sin_table).astype(jnp.bfloat16)
    new_values = proj_all[:, 2].astype(jnp.bfloat16)
    req_ends = jnp.cumsum(req_blocks)
    block_ids = jnp.arange(BLOCKS, dtype=jnp.int32)
    blk_req = lax.optimization_barrier(jnp.sum((block_ids[:, None] >= req_ends[None, :]).astype(jnp.int32), axis=1)).astype(jnp.int32)
    is_kept = keep_list == 1
    slot_index = jnp.where(is_kept, dest_slot, SLOTS).astype(jnp.int32)
    packed_keys = jnp.zeros((SLOTS + 1, ROWS, width), jnp.bfloat16).at[slot_index].set(key_cache)[:SLOTS]
    packed_values = jnp.zeros((SLOTS + 1, ROWS, width), jnp.bfloat16).at[slot_index].set(value_cache)[:SLOTS]
    packed_request = jnp.full((SLOTS + 1,), -1, jnp.int32).at[slot_index].set(blk_req)[:SLOTS]
    fold_keys, fold_values = lax.map(fold_block, (fold_weight, key_cache, value_cache))
    folded_keys = jnp.where(is_kept[:, None], 0.0, fold_keys).astype(jnp.bfloat16)
    folded_values = jnp.where(is_kept[:, None], 0.0, fold_values).astype(jnp.bfloat16)
    row_req = jnp.concatenate([jnp.repeat(packed_request, ROWS), jnp.where(is_kept, -1, blk_req).astype(jnp.int32), jnp.arange(REQS, dtype=jnp.int32)])
    segment = jnp.where(row_req >= 0, row_req, REQS).astype(jnp.int32)
    bias = jnp.concatenate([jnp.zeros((SLOTS * ROWS,), jnp.float32), jnp.full((BLOCKS,), math.log(ROWS), jnp.float32), jnp.zeros((REQS,), jnp.float32)])
    all_keys = jnp.concatenate([packed_keys.reshape(SLOTS * ROWS, HEADS, HDIM), folded_keys.reshape(BLOCKS, HEADS, HDIM), new_keys], axis=0)
    all_values = jnp.concatenate([packed_values.reshape(SLOTS * ROWS, HEADS, HDIM), folded_values.reshape(BLOCKS, HEADS, HDIM), new_values], axis=0)
    pick_rows = jnp.minimum(segment, REQS - 1)

    def head_mix(inputs):
        query_head, keys_head, values_head = inputs
        gathered = query_head[pick_rows]
        scores = lax.optimization_barrier(jnp.sum(gathered.astype(jnp.float32) * keys_head.astype(jnp.float32), axis=1)) * 0.125 + bias
        tops = jax.ops.segment_max(scores, segment, REQS + 1)
        expo = jnp.exp(scores - tops[segment])
        sums = jax.ops.segment_sum(expo, segment, REQS + 1)
        probs = lax.optimization_barrier(expo.astype(jnp.bfloat16)).astype(jnp.float32)
        weighted = jax.ops.segment_sum(probs[:, None] * values_head.astype(jnp.float32), segment, REQS + 1)
        return weighted[:REQS] / sums[:REQS, None]
    mixture = lax.map(head_mix, (jnp.transpose(queries, (1, 0, 2)), jnp.transpose(all_keys, (1, 0, 2)), jnp.transpose(all_values, (1, 0, 2))))
    mixed = jnp.transpose(mixture, (1, 0, 2)).reshape(REQS, width).astype(jnp.bfloat16)
    attn_out = jnp.dot(mixed, w_out, preferred_element_type=jnp.float32).astype(jnp.bfloat16)
    return (packed_keys, packed_values, packed_request, folded_keys, folded_values, attn_out)
```

```python
import math

import jax
import jax.numpy as jnp
from jax import lax
from jax.sharding import Mesh
from jax.sharding import PartitionSpec as P

D = 2048
HDIM = 64
ROWS = 128
HOPS = 4
CAP = 4
SLOT_DEV = 16


ROPE_BASE = 130000.0
NORM_EPSILON = 1e-05
MASKED_SCORE = -1e30

SEQ_PARTS = ("z", "x", "core")


AXIS_SIZES = {"heads": 4, "z": 8, "x": 4, "core": 2}


def exchange_steps(axes):
    for axis in axes:
        bit = 1
        while bit < AXIS_SIZES[axis]:
            yield axis, [(i, i ^ bit) for i in range(AXIS_SIZES[axis])]
            bit *= 2


def butterfly(x, merge, axes):
    for axis, pairs in exchange_steps(axes):
        x = merge(x, lax.ppermute(x, axis, pairs))
    return x


def seq_sum(x):
    return butterfly(x, jnp.add, reversed(SEQ_PARTS))


def softmax_merge(mine, theirs):
    top_a, top_b = mine[..., -1:], theirs[..., -1:]
    top = jnp.maximum(top_a, top_b)
    scale_a = jnp.exp(top_a - top)
    scale_b = jnp.exp(top_b - top)
    merged = mine[..., :-1] * scale_a + theirs[..., :-1] * scale_b
    return jnp.concatenate([merged, top], axis=-1)


def seq_index():
    index = lax.axis_index(SEQ_PARTS[0])
    for axis in SEQ_PARTS[1:]:
        index = index * lax.axis_size(axis) + lax.axis_index(axis)
    return index


def seq_size():
    count = 1
    for axis in SEQ_PARTS:
        count *= lax.axis_size(axis)
    return count


def passed_along(array, by):
    count = seq_size()
    return lax.ppermute(array, SEQ_PARTS, [(i, (i + by) % count) for i in range(count)])


def rotate_half(values, cos_table, sin_table):
    half = values.shape[-1] // 2
    lower = values[..., :half]
    upper = values[..., half:]
    return jnp.concatenate(
        [lower * cos_table - upper * sin_table, upper * cos_table + lower * sin_table], axis=-1
    )


def rope_tables(positions, head_size):
    half = head_size // 2
    freqs = ROPE_BASE ** (-(2.0 * jnp.arange(half, dtype=jnp.float32)) / head_size)
    angles = positions.astype(jnp.float32)[:, None] * freqs[None, :]
    return (jnp.cos(angles)[:, None, :], jnp.sin(angles)[:, None, :])


def shards(
    hidden,
    w_qkv,
    w_out,
    positions,
    req_blocks,
    keep_list,
    dest_slot,
    key_cache,
    value_cache,
    fold_weight,
):
    requests = hidden.shape[0]
    n_blocks, row_count, feat_width = key_cache.shape
    heads_here = feat_width // HDIM
    seq_count = seq_size()
    my_index = seq_index()

    widened = hidden.astype(jnp.float32)
    total_sq = seq_sum(jnp.sum(widened * widened, axis=1))
    normed = (widened * lax.rsqrt(total_sq / D + NORM_EPSILON)[:, None]).astype(jnp.bfloat16)
    partial_value = jnp.dot(
        normed, w_qkv.reshape(w_qkv.shape[0], 3 * feat_width), preferred_element_type=jnp.float32
    )
    proj_all = seq_sum(partial_value).reshape(requests, 3, heads_here, HDIM)
    cos_table, sin_table = rope_tables(positions, HDIM)
    queries = rotate_half(proj_all[:, 0], cos_table, sin_table).astype(jnp.bfloat16)
    new_keys = rotate_half(proj_all[:, 1], cos_table, sin_table).astype(jnp.bfloat16)
    new_values = proj_all[:, 2].astype(jnp.bfloat16)

    block_ids = jnp.arange(n_blocks, dtype=jnp.int32)
    global_ids = my_index * n_blocks + block_ids
    req_ends = jnp.cumsum(req_blocks)
    blk_req = jnp.sum((global_ids[:, None] >= req_ends[None, :]).astype(jnp.int32), axis=1)
    is_kept = keep_list == 1

    weight_sum = jnp.sum(fold_weight, axis=1)
    fold_keys = jnp.einsum(
        "bi,bif->bf",
        fold_weight,
        key_cache,
        preferred_element_type=jnp.float32,
        precision=lax.Precision.HIGHEST,
    )
    fold_values = jnp.einsum(
        "bi,bif->bf",
        fold_weight,
        value_cache,
        preferred_element_type=jnp.float32,
        precision=lax.Precision.HIGHEST,
    )
    folded_keys = jnp.where(is_kept[:, None], 0.0, fold_keys / weight_sum[:, None]).astype(
        jnp.bfloat16
    )
    folded_values = jnp.where(is_kept[:, None], 0.0, fold_values / weight_sum[:, None]).astype(
        jnp.bfloat16
    )

    owners = dest_slot // SLOT_DEV
    local_slot = dest_slot % SLOT_DEV
    hop_of = (owners - my_index) % seq_count
    earlier = (
        is_kept[None, :]
        & is_kept[:, None]
        & (hop_of[None, :] == hop_of[:, None])
        & (block_ids[None, :] < block_ids[:, None])
    )
    placed = jnp.sum(earlier.astype(jnp.int32), axis=1)
    arrivals = HOPS * CAP
    send_pos = jnp.where(is_kept, hop_of * CAP + placed, arrivals)
    targets = jnp.arange(arrivals, dtype=jnp.int32)
    hit_table = send_pos[None, :] == targets[:, None]
    has_block = jnp.any(hit_table, axis=1)
    source = jnp.sum(jnp.where(hit_table, block_ids[None, :], 0), axis=1)
    send_keys = key_cache[source].reshape(HOPS, CAP, row_count, feat_width)
    send_values = value_cache[source].reshape(HOPS, CAP, row_count, feat_width)
    meta_data = jnp.stack(
        [jnp.where(has_block, local_slot[source], -1), jnp.where(has_block, blk_req[source], -1)],
        axis=-1,
    )
    meta_data = meta_data.astype(jnp.float32).astype(jnp.bfloat16).reshape(HOPS, CAP, 2)
    arrived = [(send_keys[0], send_values[0], meta_data[0])]
    for distance in range(1, HOPS):
        arrived.append(
            passed_along((send_keys[distance], send_values[distance], meta_data[distance]), distance)
        )
    recv_keys = jnp.stack([entry[0] for entry in arrived])
    recv_values = jnp.stack([entry[1] for entry in arrived])
    recv_meta = jnp.stack([entry[2] for entry in arrived])
    recv_keys = recv_keys.reshape(arrivals, row_count, feat_width)
    recv_values = recv_values.reshape(arrivals, row_count, feat_width)
    recv_meta = recv_meta.reshape(arrivals, 2).astype(jnp.float32).astype(jnp.int32)
    match_table = recv_meta[None, :, 0] == jnp.arange(SLOT_DEV, dtype=jnp.int32)[:, None]
    filled = jnp.any(match_table, axis=1)
    picked = jnp.sum(
        jnp.where(match_table, jnp.arange(arrivals, dtype=jnp.int32)[None, :], 0), axis=1
    )
    packed_keys = jnp.where(filled[:, None, None], recv_keys[picked], jnp.zeros((), jnp.bfloat16))
    packed_values = jnp.where(
        filled[:, None, None], recv_values[picked], jnp.zeros((), jnp.bfloat16)
    )
    packed_request = jnp.where(filled, recv_meta[picked, 1], -1)

    row_keys = key_cache.reshape(-1, heads_here, HDIM)
    row_values = value_cache.reshape(-1, heads_here, HDIM)
    row_req = jnp.repeat(jnp.where(is_kept, blk_req, -1), row_count)
    all_keys = jnp.concatenate([row_keys, folded_keys.reshape(n_blocks, heads_here, HDIM)], axis=0)
    all_values = jnp.concatenate(
        [row_values, folded_values.reshape(n_blocks, heads_here, HDIM)], axis=0
    )
    all_req = jnp.concatenate([row_req, jnp.where(is_kept, -1, blk_req)])
    bias = jnp.concatenate(
        [
            jnp.zeros((row_req.shape[0],), jnp.float32),
            jnp.full((n_blocks,), math.log(ROWS), jnp.float32),
        ]
    )
    row_mask = all_req[None, :] == jnp.arange(requests, dtype=jnp.int32)[:, None]
    scores = (
        jnp.einsum("rhd,nhd->hrn", queries, all_keys, preferred_element_type=jnp.float32) * 0.125
        + bias[None, None, :]
    )
    scores = jnp.where(row_mask[None], scores, MASKED_SCORE)
    local_top = jnp.max(scores, axis=2)
    expo = jnp.where(row_mask[None], jnp.exp(scores - local_top[..., None]), 0.0)
    local_sum = jnp.sum(expo, axis=2)
    local_acc = jnp.einsum(
        "hrn,nhd->hrd", expo.astype(jnp.bfloat16), all_values, preferred_element_type=jnp.float32
    )
    stats = jnp.concatenate(
        [local_acc, local_sum[..., None], local_top[..., None]], axis=-1
    )
    stats = butterfly(stats, softmax_merge, reversed(SEQ_PARTS))
    mixture = stats[..., :HDIM]
    totals = stats[..., HDIM]
    top_score = stats[..., HDIM + 1]
    own_score = (
        jnp.einsum("rhd,rhd->hr", queries, new_keys, preferred_element_type=jnp.float32) * 0.125
    )
    final_top = jnp.maximum(top_score, own_score)
    shrink = jnp.exp(top_score - final_top)
    own_expo = jnp.exp(own_score - final_top)
    own_prob = lax.optimization_barrier(own_expo.astype(jnp.bfloat16)).astype(jnp.float32)
    totals = totals * shrink + own_expo
    own_values = jnp.transpose(new_values, (1, 0, 2)).astype(jnp.float32)
    mixture = mixture * shrink[..., None] + own_prob[..., None] * own_values
    mixed = (mixture / totals[..., None]).astype(jnp.bfloat16)
    mixed_rows = jnp.transpose(mixed, (1, 0, 2)).reshape(requests, feat_width)
    out_terms = jnp.dot(mixed_rows, w_out, preferred_element_type=jnp.float32)
    attn_out = butterfly(out_terms, jnp.add, ["heads"]).astype(jnp.bfloat16)
    return (packed_keys, packed_values, packed_request, folded_keys, folded_values, attn_out)


def solution(mesh):
    heads_count, seq_count = mesh.devices.shape
    fine = Mesh(
        mesh.devices.reshape(heads_count, seq_count // 8, 4, 2),
        ("heads",) + SEQ_PARTS,
    )
    seq = SEQ_PARTS
    return jax.shard_map(
        shards,
        mesh=fine,
        in_specs=(
            P(None, seq),
            P(seq, None, "heads"),
            P("heads", seq),
            P(),
            P(),
            P(seq),
            P(seq),
            P(seq, None, "heads"),
            P(seq, None, "heads"),
            P(seq, None),
        ),
        out_specs=(
            P(seq, None, "heads"),
            P(seq, None, "heads"),
            P(seq),
            P(seq, "heads"),
            P(seq, "heads"),
            P(None, seq),
        ),
        check_vma=False,
    )
```

```python
import math

import jax
import jax.numpy as jnp
from jax import lax
from jax.sharding import Mesh
from jax.sharding import PartitionSpec as P

D = 2048
HDIM = 64
ROWS = 128
HOPS = 4
CAP = 4
SLOT_DEV = 16


ROPE_BASE = 130000.0
NORM_EPSILON = 1e-05
MASKED_SCORE = -1e30

SEQ_PARTS = ("z", "x", "core")


AXIS_SIZES = {"heads": 4, "z": 8, "x": 4, "core": 2}


def exchange_steps(axes):
    for axis in axes:
        bit = 1
        while bit < AXIS_SIZES[axis]:
            yield axis, [(i, i ^ bit) for i in range(AXIS_SIZES[axis])]
            bit *= 2


def butterfly(x, merge, axes):
    for axis, pairs in exchange_steps(axes):
        x = merge(x, lax.ppermute(x, axis, pairs))
    return x


def seq_sum(x):
    return butterfly(x, jnp.add, reversed(SEQ_PARTS))


def softmax_merge(mine, theirs):
    top_a, top_b = mine[..., -1:], theirs[..., -1:]
    top = jnp.maximum(top_a, top_b)
    scale_a = jnp.exp(top_a - top)
    scale_b = jnp.exp(top_b - top)
    merged = mine[..., :-1] * scale_a + theirs[..., :-1] * scale_b
    return jnp.concatenate([merged, top], axis=-1)


def seq_index():
    index = lax.axis_index(SEQ_PARTS[0])
    for axis in SEQ_PARTS[1:]:
        index = index * lax.axis_size(axis) + lax.axis_index(axis)
    return index


def seq_size():
    count = 1
    for axis in SEQ_PARTS:
        count *= lax.axis_size(axis)
    return count


def passed_along(array, by):
    count = seq_size()
    return lax.ppermute(array, SEQ_PARTS, [(i, (i + by) % count) for i in range(count)])


def rotate_half(values, cos_table, sin_table):
    half = values.shape[-1] // 2
    lower = values[..., :half]
    upper = values[..., half:]
    return jnp.concatenate(
        [lower * cos_table - upper * sin_table, upper * cos_table + lower * sin_table], axis=-1
    )


def rope_tables(positions, head_size):
    half = head_size // 2
    freqs = ROPE_BASE ** (-(2.0 * jnp.arange(half, dtype=jnp.float32)) / head_size)
    angles = positions.astype(jnp.float32)[:, None] * freqs[None, :]
    return (jnp.cos(angles)[:, None, :], jnp.sin(angles)[:, None, :])


def shards(
    hidden,
    w_qkv,
    w_out,
    positions,
    req_blocks,
    keep_list,
    dest_slot,
    key_cache,
    value_cache,
    fold_weight,
):
    requests = hidden.shape[0]
    n_blocks, row_count, feat_width = key_cache.shape
    heads_here = feat_width // HDIM
    seq_count = seq_size()
    my_index = seq_index()

    widened = hidden.astype(jnp.float32)
    total_sq = seq_sum(jnp.sum(widened * widened, axis=1))
    normed = (widened * lax.rsqrt(total_sq / D + NORM_EPSILON)[:, None]).astype(jnp.bfloat16)
    partial_value = jnp.dot(
        normed, w_qkv.reshape(w_qkv.shape[0], 3 * feat_width), preferred_element_type=jnp.float32
    )
    proj_all = seq_sum(partial_value).reshape(requests, 3, heads_here, HDIM)
    block_ids = jnp.arange(n_blocks, dtype=jnp.int32)
    global_ids = my_index * n_blocks + block_ids
    req_ends = jnp.cumsum(req_blocks)
    blk_req = jnp.sum((global_ids[:, None] >= req_ends[None, :]).astype(jnp.int32), axis=1)
    is_kept = keep_list == 1

    weight_sum = jnp.sum(fold_weight, axis=1)
    fold_keys = jnp.einsum(
        "bi,bif->bf",
        fold_weight,
        key_cache,
        preferred_element_type=jnp.float32,
        precision=lax.Precision.HIGHEST,
    )
    fold_values = jnp.einsum(
        "bi,bif->bf",
        fold_weight,
        value_cache,
        preferred_element_type=jnp.float32,
        precision=lax.Precision.HIGHEST,
    )
    folded_keys = jnp.where(is_kept[:, None], 0.0, fold_keys / weight_sum[:, None]).astype(
        jnp.bfloat16
    )
    folded_values = jnp.where(is_kept[:, None], 0.0, fold_values / weight_sum[:, None]).astype(
        jnp.bfloat16
    )

    owners = dest_slot // SLOT_DEV
    local_slot = dest_slot % SLOT_DEV
    hop_of = (owners - my_index) % seq_count
    earlier = (
        is_kept[None, :]
        & is_kept[:, None]
        & (hop_of[None, :] == hop_of[:, None])
        & (block_ids[None, :] < block_ids[:, None])
    )
    placed = jnp.sum(earlier.astype(jnp.int32), axis=1)
    arrivals = HOPS * CAP
    send_pos = jnp.where(is_kept, hop_of * CAP + placed, arrivals)
    targets = jnp.arange(arrivals, dtype=jnp.int32)
    hit_table = send_pos[None, :] == targets[:, None]
    has_block = jnp.any(hit_table, axis=1)
    source = jnp.sum(jnp.where(hit_table, block_ids[None, :], 0), axis=1)
    send_keys = key_cache[source].reshape(HOPS, CAP, row_count, feat_width)
    send_values = value_cache[source].reshape(HOPS, CAP, row_count, feat_width)
    meta_data = jnp.stack(
        [jnp.where(has_block, local_slot[source], -1), jnp.where(has_block, blk_req[source], -1)],
        axis=-1,
    )
    meta_data = meta_data.astype(jnp.float32).astype(jnp.bfloat16).reshape(HOPS, CAP, 2)
    send_keys, send_values, meta_data, proj_all = lax.optimization_barrier(
        (send_keys, send_values, meta_data, proj_all)
    )
    arrived = [(send_keys[0], send_values[0], meta_data[0])]
    for distance in range(1, HOPS):
        arrived.append(
            passed_along((send_keys[distance], send_values[distance], meta_data[distance]), distance)
        )
    recv_keys = jnp.stack([entry[0] for entry in arrived])
    recv_values = jnp.stack([entry[1] for entry in arrived])
    recv_meta = jnp.stack([entry[2] for entry in arrived])
    recv_keys = recv_keys.reshape(arrivals, row_count, feat_width)
    recv_values = recv_values.reshape(arrivals, row_count, feat_width)
    recv_meta = recv_meta.reshape(arrivals, 2).astype(jnp.float32).astype(jnp.int32)
    match_table = recv_meta[None, :, 0] == jnp.arange(SLOT_DEV, dtype=jnp.int32)[:, None]
    filled = jnp.any(match_table, axis=1)
    picked = jnp.sum(
        jnp.where(match_table, jnp.arange(arrivals, dtype=jnp.int32)[None, :], 0), axis=1
    )
    packed_keys = jnp.where(filled[:, None, None], recv_keys[picked], jnp.zeros((), jnp.bfloat16))
    packed_values = jnp.where(
        filled[:, None, None], recv_values[picked], jnp.zeros((), jnp.bfloat16)
    )
    packed_request = jnp.where(filled, recv_meta[picked, 1], -1)

    cos_table, sin_table = rope_tables(positions, HDIM)
    queries = rotate_half(proj_all[:, 0], cos_table, sin_table).astype(jnp.bfloat16)
    new_keys = rotate_half(proj_all[:, 1], cos_table, sin_table).astype(jnp.bfloat16)
    new_values = proj_all[:, 2].astype(jnp.bfloat16)

    row_keys = key_cache.reshape(-1, heads_here, HDIM)
    row_values = value_cache.reshape(-1, heads_here, HDIM)
    row_req = jnp.repeat(jnp.where(is_kept, blk_req, -1), row_count)
    all_keys = jnp.concatenate([row_keys, folded_keys.reshape(n_blocks, heads_here, HDIM)], axis=0)
    all_values = jnp.concatenate(
        [row_values, folded_values.reshape(n_blocks, heads_here, HDIM)], axis=0
    )
    all_req = jnp.concatenate([row_req, jnp.where(is_kept, -1, blk_req)])
    bias = jnp.concatenate(
        [
            jnp.zeros((row_req.shape[0],), jnp.float32),
            jnp.full((n_blocks,), math.log(ROWS), jnp.float32),
        ]
    )
    row_mask = all_req[None, :] == jnp.arange(requests, dtype=jnp.int32)[:, None]
    scores = (
        jnp.einsum("rhd,nhd->hrn", queries, all_keys, preferred_element_type=jnp.float32) * 0.125
        + bias[None, None, :]
    )
    scores = jnp.where(row_mask[None], scores, MASKED_SCORE)
    local_top = jnp.max(scores, axis=2)
    expo = jnp.where(row_mask[None], jnp.exp(scores - local_top[..., None]), 0.0)
    local_sum = jnp.sum(expo, axis=2)
    local_acc = jnp.einsum(
        "hrn,nhd->hrd", expo.astype(jnp.bfloat16), all_values, preferred_element_type=jnp.float32
    )
    stats = jnp.concatenate(
        [local_acc, local_sum[..., None], local_top[..., None]], axis=-1
    )
    recv_keys, recv_values, recv_meta, stats = lax.optimization_barrier(
        (recv_keys, recv_values, recv_meta, stats)
    )
    stats = butterfly(stats, softmax_merge, reversed(SEQ_PARTS))
    mixture = stats[..., :HDIM]
    totals = stats[..., HDIM]
    top_score = stats[..., HDIM + 1]
    own_score = (
        jnp.einsum("rhd,rhd->hr", queries, new_keys, preferred_element_type=jnp.float32) * 0.125
    )
    final_top = jnp.maximum(top_score, own_score)
    shrink = jnp.exp(top_score - final_top)
    own_expo = jnp.exp(own_score - final_top)
    own_prob = lax.optimization_barrier(own_expo.astype(jnp.bfloat16)).astype(jnp.float32)
    totals = totals * shrink + own_expo
    own_values = jnp.transpose(new_values, (1, 0, 2)).astype(jnp.float32)
    mixture = mixture * shrink[..., None] + own_prob[..., None] * own_values
    mixed = (mixture / totals[..., None]).astype(jnp.bfloat16)
    mixed_rows = jnp.transpose(mixed, (1, 0, 2)).reshape(requests, feat_width)
    out_terms = jnp.dot(mixed_rows, w_out, preferred_element_type=jnp.float32)
    attn_out = butterfly(out_terms, jnp.add, ["heads"]).astype(jnp.bfloat16)
    return (packed_keys, packed_values, packed_request, folded_keys, folded_values, attn_out)


def solution(mesh):
    heads_count, seq_count = mesh.devices.shape
    fine = Mesh(
        mesh.devices.reshape(heads_count, seq_count // 8, 4, 2),
        ("heads",) + SEQ_PARTS,
    )
    seq = SEQ_PARTS
    return jax.shard_map(
        shards,
        mesh=fine,
        in_specs=(
            P(None, seq),
            P(seq, None, "heads"),
            P("heads", seq),
            P(),
            P(),
            P(seq),
            P(seq),
            P(seq, None, "heads"),
            P(seq, None, "heads"),
            P(seq, None),
        ),
        out_specs=(
            P(seq, None, "heads"),
            P(seq, None, "heads"),
            P(seq),
            P(seq, "heads"),
            P(seq, "heads"),
            P(None, seq),
        ),
        check_vma=False,
    )
```

```python
import math

import jax
import jax.numpy as jnp
from jax import lax
from jax.sharding import Mesh
from jax.sharding import PartitionSpec as P

D = 2048
HDIM = 64
ROWS = 128
HOPS = 4
CAP = 4
SLOT_DEV = 16


ROPE_BASE = 130000.0
NORM_EPSILON = 1e-05
MASKED_SCORE = -1e30

SEQ_PARTS = ("z", "x", "core")


AXIS_SIZES = {"heads": 4, "z": 8, "x": 4, "core": 2}


def exchange_steps(axes):
    for axis in axes:
        bit = 1
        while bit < AXIS_SIZES[axis]:
            yield axis, [(i, i ^ bit) for i in range(AXIS_SIZES[axis])]
            bit *= 2


def butterfly(x, merge, axes):
    for axis, pairs in exchange_steps(axes):
        x = merge(x, lax.ppermute(x, axis, pairs))
    return x


def seq_sum(x):
    return butterfly(x, jnp.add, reversed(SEQ_PARTS))


def softmax_merge(mine, theirs):
    top_a, top_b = mine[..., -1:], theirs[..., -1:]
    top = jnp.maximum(top_a, top_b)
    scale_a = jnp.exp(top_a - top)
    scale_b = jnp.exp(top_b - top)
    merged = mine[..., :-1] * scale_a + theirs[..., :-1] * scale_b
    return jnp.concatenate([merged, top], axis=-1)


def seq_index():
    index = lax.axis_index(SEQ_PARTS[0])
    for axis in SEQ_PARTS[1:]:
        index = index * lax.axis_size(axis) + lax.axis_index(axis)
    return index


def seq_size():
    count = 1
    for axis in SEQ_PARTS:
        count *= lax.axis_size(axis)
    return count


def passed_along(array, by):
    count = seq_size()
    return lax.ppermute(array, SEQ_PARTS, [(i, (i + by) % count) for i in range(count)])


def rotate_half(values, cos_table, sin_table):
    half = values.shape[-1] // 2
    lower = values[..., :half]
    upper = values[..., half:]
    return jnp.concatenate(
        [lower * cos_table - upper * sin_table, upper * cos_table + lower * sin_table], axis=-1
    )


def rope_tables(positions, head_size):
    half = head_size // 2
    freqs = ROPE_BASE ** (-(2.0 * jnp.arange(half, dtype=jnp.float32)) / head_size)
    angles = positions.astype(jnp.float32)[:, None] * freqs[None, :]
    return (jnp.cos(angles)[:, None, :], jnp.sin(angles)[:, None, :])


def shards(
    hidden,
    w_qkv,
    w_out,
    positions,
    req_blocks,
    keep_list,
    dest_slot,
    key_cache,
    value_cache,
    fold_weight,
):
    requests = hidden.shape[0]
    n_blocks, row_count, feat_width = key_cache.shape
    heads_here = feat_width // HDIM
    seq_count = seq_size()
    my_index = seq_index()

    widened = hidden.astype(jnp.float32)
    total_sq = seq_sum(jnp.sum(widened * widened, axis=1))
    normed = (widened * lax.rsqrt(total_sq / D + NORM_EPSILON)[:, None]).astype(jnp.bfloat16)
    partial_value = jnp.dot(
        normed, w_qkv.reshape(w_qkv.shape[0], 3 * feat_width), preferred_element_type=jnp.float32
    )
    block_ids = jnp.arange(n_blocks, dtype=jnp.int32)
    global_ids = my_index * n_blocks + block_ids
    req_ends = jnp.cumsum(req_blocks)
    blk_req = jnp.sum((global_ids[:, None] >= req_ends[None, :]).astype(jnp.int32), axis=1)
    is_kept = keep_list == 1

    weight_sum = jnp.sum(fold_weight, axis=1)
    fold_keys = jnp.einsum(
        "bi,bif->bf",
        fold_weight,
        key_cache,
        preferred_element_type=jnp.float32,
        precision=lax.Precision.HIGHEST,
    )
    fold_values = jnp.einsum(
        "bi,bif->bf",
        fold_weight,
        value_cache,
        preferred_element_type=jnp.float32,
        precision=lax.Precision.HIGHEST,
    )
    folded_keys = jnp.where(is_kept[:, None], 0.0, fold_keys / weight_sum[:, None]).astype(
        jnp.bfloat16
    )
    folded_values = jnp.where(is_kept[:, None], 0.0, fold_values / weight_sum[:, None]).astype(
        jnp.bfloat16
    )

    owners = dest_slot // SLOT_DEV
    local_slot = dest_slot % SLOT_DEV
    hop_of = (owners - my_index) % seq_count
    earlier = (
        is_kept[None, :]
        & is_kept[:, None]
        & (hop_of[None, :] == hop_of[:, None])
        & (block_ids[None, :] < block_ids[:, None])
    )
    placed = jnp.sum(earlier.astype(jnp.int32), axis=1)
    arrivals = HOPS * CAP
    send_pos = jnp.where(is_kept, hop_of * CAP + placed, arrivals)
    targets = jnp.arange(arrivals, dtype=jnp.int32)
    hit_table = send_pos[None, :] == targets[:, None]
    has_block = jnp.any(hit_table, axis=1)
    source = jnp.sum(jnp.where(hit_table, block_ids[None, :], 0), axis=1)
    send_keys = key_cache[source].reshape(HOPS, CAP, row_count, feat_width)
    send_values = value_cache[source].reshape(HOPS, CAP, row_count, feat_width)
    meta_data = jnp.stack(
        [jnp.where(has_block, local_slot[source], -1), jnp.where(has_block, blk_req[source], -1)],
        axis=-1,
    )
    meta_data = meta_data.astype(jnp.float32).astype(jnp.bfloat16).reshape(HOPS, CAP, 2)
    send_keys, send_values, meta_data, partial_value = lax.optimization_barrier(
        (send_keys, send_values, meta_data, partial_value)
    )
    proj_all = seq_sum(partial_value).reshape(requests, 3, heads_here, HDIM)
    arrived = [(send_keys[0], send_values[0], meta_data[0])]
    for distance in range(1, HOPS):
        arrived.append(
            passed_along((send_keys[distance], send_values[distance], meta_data[distance]), distance)
        )
    recv_keys = jnp.stack([entry[0] for entry in arrived])
    recv_values = jnp.stack([entry[1] for entry in arrived])
    recv_meta = jnp.stack([entry[2] for entry in arrived])
    recv_keys = recv_keys.reshape(arrivals, row_count, feat_width)
    recv_values = recv_values.reshape(arrivals, row_count, feat_width)
    recv_meta = recv_meta.reshape(arrivals, 2).astype(jnp.float32).astype(jnp.int32)
    match_table = recv_meta[None, :, 0] == jnp.arange(SLOT_DEV, dtype=jnp.int32)[:, None]
    filled = jnp.any(match_table, axis=1)
    picked = jnp.sum(
        jnp.where(match_table, jnp.arange(arrivals, dtype=jnp.int32)[None, :], 0), axis=1
    )
    packed_keys = jnp.where(filled[:, None, None], recv_keys[picked], jnp.zeros((), jnp.bfloat16))
    packed_values = jnp.where(
        filled[:, None, None], recv_values[picked], jnp.zeros((), jnp.bfloat16)
    )
    packed_request = jnp.where(filled, recv_meta[picked, 1], -1)

    recv_keys, recv_values, recv_meta, proj_all = lax.optimization_barrier(
        (recv_keys, recv_values, recv_meta, proj_all)
    )
    cos_table, sin_table = rope_tables(positions, HDIM)
    queries = rotate_half(proj_all[:, 0], cos_table, sin_table).astype(jnp.bfloat16)
    new_keys = rotate_half(proj_all[:, 1], cos_table, sin_table).astype(jnp.bfloat16)
    new_values = proj_all[:, 2].astype(jnp.bfloat16)

    row_keys = key_cache.reshape(-1, heads_here, HDIM)
    row_values = value_cache.reshape(-1, heads_here, HDIM)
    row_req = jnp.repeat(jnp.where(is_kept, blk_req, -1), row_count)
    all_keys = jnp.concatenate([row_keys, folded_keys.reshape(n_blocks, heads_here, HDIM)], axis=0)
    all_values = jnp.concatenate(
        [row_values, folded_values.reshape(n_blocks, heads_here, HDIM)], axis=0
    )
    all_req = jnp.concatenate([row_req, jnp.where(is_kept, -1, blk_req)])
    bias = jnp.concatenate(
        [
            jnp.zeros((row_req.shape[0],), jnp.float32),
            jnp.full((n_blocks,), math.log(ROWS), jnp.float32),
        ]
    )
    row_mask = all_req[None, :] == jnp.arange(requests, dtype=jnp.int32)[:, None]
    scores = (
        jnp.einsum("rhd,nhd->hrn", queries, all_keys, preferred_element_type=jnp.float32) * 0.125
        + bias[None, None, :]
    )
    scores = jnp.where(row_mask[None], scores, MASKED_SCORE)
    local_top = jnp.max(scores, axis=2)
    expo = jnp.where(row_mask[None], jnp.exp(scores - local_top[..., None]), 0.0)
    local_sum = jnp.sum(expo, axis=2)
    local_acc = jnp.einsum(
        "hrn,nhd->hrd", expo.astype(jnp.bfloat16), all_values, preferred_element_type=jnp.float32
    )
    stats = jnp.concatenate(
        [local_acc, local_sum[..., None], local_top[..., None]], axis=-1
    )
    stats = butterfly(stats, softmax_merge, reversed(SEQ_PARTS))
    mixture = stats[..., :HDIM]
    totals = stats[..., HDIM]
    top_score = stats[..., HDIM + 1]
    own_score = (
        jnp.einsum("rhd,rhd->hr", queries, new_keys, preferred_element_type=jnp.float32) * 0.125
    )
    final_top = jnp.maximum(top_score, own_score)
    shrink = jnp.exp(top_score - final_top)
    own_expo = jnp.exp(own_score - final_top)
    own_prob = lax.optimization_barrier(own_expo.astype(jnp.bfloat16)).astype(jnp.float32)
    totals = totals * shrink + own_expo
    own_values = jnp.transpose(new_values, (1, 0, 2)).astype(jnp.float32)
    mixture = mixture * shrink[..., None] + own_prob[..., None] * own_values
    mixed = (mixture / totals[..., None]).astype(jnp.bfloat16)
    mixed_rows = jnp.transpose(mixed, (1, 0, 2)).reshape(requests, feat_width)
    out_terms = jnp.dot(mixed_rows, w_out, preferred_element_type=jnp.float32)
    attn_out = butterfly(out_terms, jnp.add, ["heads"]).astype(jnp.bfloat16)
    return (packed_keys, packed_values, packed_request, folded_keys, folded_values, attn_out)


def solution(mesh):
    heads_count, seq_count = mesh.devices.shape
    fine = Mesh(
        mesh.devices.reshape(heads_count, seq_count // 8, 4, 2),
        ("heads",) + SEQ_PARTS,
    )
    seq = SEQ_PARTS
    return jax.shard_map(
        shards,
        mesh=fine,
        in_specs=(
            P(None, seq),
            P(seq, None, "heads"),
            P("heads", seq),
            P(),
            P(),
            P(seq),
            P(seq),
            P(seq, None, "heads"),
            P(seq, None, "heads"),
            P(seq, None),
        ),
        out_specs=(
            P(seq, None, "heads"),
            P(seq, None, "heads"),
            P(seq),
            P(seq, "heads"),
            P(seq, "heads"),
            P(None, seq),
        ),
        check_vma=False,
    )
```

```python
import math

import jax
import jax.numpy as jnp
from jax import lax
from jax.sharding import Mesh
from jax.sharding import PartitionSpec as P

D = 2048
HDIM = 64
ROWS = 128
HOPS = 4
CAP = 4
SLOT_DEV = 16


ROPE_BASE = 130000.0
NORM_EPSILON = 1e-05
MASKED_SCORE = -1e30

SEQ_PARTS = ("z", "x", "core")


AXIS_SIZES = {"heads": 4, "z": 8, "x": 4, "core": 2}


def exchange_steps(axes):
    for axis in axes:
        bit = 1
        while bit < AXIS_SIZES[axis]:
            yield axis, [(i, i ^ bit) for i in range(AXIS_SIZES[axis])]
            bit *= 2


def butterfly(x, merge, axes):
    for axis, pairs in exchange_steps(axes):
        x = merge(x, lax.ppermute(x, axis, pairs))
    return x


def seq_sum(x):
    return butterfly(x, jnp.add, reversed(SEQ_PARTS))


def softmax_merge(mine, theirs):
    top_a, top_b = mine[..., -1:], theirs[..., -1:]
    top = jnp.maximum(top_a, top_b)
    scale_a = jnp.exp(top_a - top)
    scale_b = jnp.exp(top_b - top)
    merged = mine[..., :-1] * scale_a + theirs[..., :-1] * scale_b
    return jnp.concatenate([merged, top], axis=-1)


def seq_index():
    index = lax.axis_index(SEQ_PARTS[0])
    for axis in SEQ_PARTS[1:]:
        index = index * lax.axis_size(axis) + lax.axis_index(axis)
    return index


def seq_size():
    count = 1
    for axis in SEQ_PARTS:
        count *= lax.axis_size(axis)
    return count


def passed_along(array, by):
    count = seq_size()
    return lax.ppermute(array, SEQ_PARTS, [(i, (i + by) % count) for i in range(count)])


def rotate_half(values, cos_table, sin_table):
    half = values.shape[-1] // 2
    lower = values[..., :half]
    upper = values[..., half:]
    return jnp.concatenate(
        [lower * cos_table - upper * sin_table, upper * cos_table + lower * sin_table], axis=-1
    )


def rope_tables(positions, head_size):
    half = head_size // 2
    freqs = ROPE_BASE ** (-(2.0 * jnp.arange(half, dtype=jnp.float32)) / head_size)
    angles = positions.astype(jnp.float32)[:, None] * freqs[None, :]
    return (jnp.cos(angles)[:, None, :], jnp.sin(angles)[:, None, :])


def shards(
    hidden,
    w_qkv,
    w_out,
    positions,
    req_blocks,
    keep_list,
    dest_slot,
    key_cache,
    value_cache,
    fold_weight,
):
    requests = hidden.shape[0]
    n_blocks, row_count, feat_width = key_cache.shape
    heads_here = feat_width // HDIM
    seq_count = seq_size()
    my_index = seq_index()

    widened = hidden.astype(jnp.float32)
    total_sq = seq_sum(jnp.sum(widened * widened, axis=1))
    normed = (widened * lax.rsqrt(total_sq / D + NORM_EPSILON)[:, None]).astype(jnp.bfloat16)
    partial_value = jnp.dot(
        normed, w_qkv.reshape(w_qkv.shape[0], 3 * feat_width), preferred_element_type=jnp.float32
    )
    proj_all = seq_sum(partial_value).reshape(requests, 3, heads_here, HDIM)
    cos_table, sin_table = rope_tables(positions, HDIM)
    queries = rotate_half(proj_all[:, 0], cos_table, sin_table).astype(jnp.bfloat16)
    new_keys = rotate_half(proj_all[:, 1], cos_table, sin_table).astype(jnp.bfloat16)
    new_values = proj_all[:, 2].astype(jnp.bfloat16)

    block_ids = jnp.arange(n_blocks, dtype=jnp.int32)
    global_ids = my_index * n_blocks + block_ids
    req_ends = jnp.cumsum(req_blocks)
    blk_req = jnp.sum((global_ids[:, None] >= req_ends[None, :]).astype(jnp.int32), axis=1)
    is_kept = keep_list == 1

    weight_sum = jnp.sum(fold_weight, axis=1)
    fold_keys = jnp.einsum(
        "bi,bif->bf",
        fold_weight,
        key_cache,
        preferred_element_type=jnp.float32,
        precision=lax.Precision.HIGHEST,
    )
    fold_values = jnp.einsum(
        "bi,bif->bf",
        fold_weight,
        value_cache,
        preferred_element_type=jnp.float32,
        precision=lax.Precision.HIGHEST,
    )
    folded_keys = jnp.where(is_kept[:, None], 0.0, fold_keys / weight_sum[:, None]).astype(
        jnp.bfloat16
    )
    folded_values = jnp.where(is_kept[:, None], 0.0, fold_values / weight_sum[:, None]).astype(
        jnp.bfloat16
    )

    owners = dest_slot // SLOT_DEV
    local_slot = dest_slot % SLOT_DEV
    hop_of = (owners - my_index) % seq_count
    earlier = (
        is_kept[None, :]
        & is_kept[:, None]
        & (hop_of[None, :] == hop_of[:, None])
        & (block_ids[None, :] < block_ids[:, None])
    )
    placed = jnp.sum(earlier.astype(jnp.int32), axis=1)
    arrivals = HOPS * CAP
    send_pos = jnp.where(is_kept, hop_of * CAP + placed, arrivals)
    targets = jnp.arange(arrivals, dtype=jnp.int32)
    hit_table = send_pos[None, :] == targets[:, None]
    has_block = jnp.any(hit_table, axis=1)
    source = jnp.sum(jnp.where(hit_table, block_ids[None, :], 0), axis=1)
    send_keys = key_cache[source].reshape(HOPS, CAP, row_count, feat_width)
    send_values = value_cache[source].reshape(HOPS, CAP, row_count, feat_width)
    meta_data = jnp.stack(
        [jnp.where(has_block, local_slot[source], -1), jnp.where(has_block, blk_req[source], -1)],
        axis=-1,
    )
    meta_data = meta_data.astype(jnp.float32).astype(jnp.bfloat16).reshape(HOPS, CAP, 2)
    arrived = [(send_keys[0], send_values[0], meta_data[0])]
    for distance in range(1, HOPS):
        arrived.append(
            passed_along((send_keys[distance], send_values[distance], meta_data[distance]), distance)
        )
    recv_keys = jnp.stack([entry[0] for entry in arrived])
    recv_values = jnp.stack([entry[1] for entry in arrived])
    recv_meta = jnp.stack([entry[2] for entry in arrived])
    recv_keys = recv_keys.reshape(arrivals, row_count, feat_width)
    recv_values = recv_values.reshape(arrivals, row_count, feat_width)
    recv_meta = recv_meta.reshape(arrivals, 2).astype(jnp.float32).astype(jnp.int32)
    match_table = recv_meta[None, :, 0] == jnp.arange(SLOT_DEV, dtype=jnp.int32)[:, None]
    filled = jnp.any(match_table, axis=1)
    picked = jnp.sum(
        jnp.where(match_table, jnp.arange(arrivals, dtype=jnp.int32)[None, :], 0), axis=1
    )
    packed_keys = jnp.where(filled[:, None, None], recv_keys[picked], jnp.zeros((), jnp.bfloat16))
    packed_values = jnp.where(
        filled[:, None, None], recv_values[picked], jnp.zeros((), jnp.bfloat16)
    )
    packed_request = jnp.where(filled, recv_meta[picked, 1], -1)

    row_keys = key_cache.reshape(-1, heads_here, HDIM)
    row_values = value_cache.reshape(-1, heads_here, HDIM)
    row_req = jnp.repeat(jnp.where(is_kept, blk_req, -1), row_count)
    all_keys = jnp.concatenate([row_keys, folded_keys.reshape(n_blocks, heads_here, HDIM)], axis=0)
    all_values = jnp.concatenate(
        [row_values, folded_values.reshape(n_blocks, heads_here, HDIM)], axis=0
    )
    all_req = jnp.concatenate([row_req, jnp.where(is_kept, -1, blk_req)])
    bias = jnp.concatenate(
        [
            jnp.zeros((row_req.shape[0],), jnp.float32),
            jnp.full((n_blocks,), math.log(ROWS), jnp.float32),
        ]
    )
    row_mask = all_req[None, :] == jnp.arange(requests, dtype=jnp.int32)[:, None]
    own_head = jnp.arange(heads_here)[:, None] == jnp.arange(heads_here)[None, :]
    spread_queries = jnp.where(
        own_head[None, :, :, None], queries[:, :, None, :], jnp.zeros((), jnp.bfloat16)
    ).reshape(requests * heads_here, feat_width)
    flat_keys = all_keys.reshape(-1, feat_width)
    flat_values = all_values.reshape(-1, feat_width)
    scores = lax.dot_general(
        spread_queries, flat_keys, (((1,), (1,)), ((), ())), preferred_element_type=jnp.float32
    ).reshape(requests, heads_here, -1)
    scores = scores * 0.125 + bias[None, None, :]
    scores = jnp.where(row_mask[:, None, :], scores, MASKED_SCORE)
    local_top = jnp.max(scores, axis=2)
    expo = jnp.where(row_mask[:, None, :], jnp.exp(scores - local_top[..., None]), 0.0)
    local_sum = jnp.sum(expo, axis=2)
    weighted = jnp.dot(
        expo.astype(jnp.bfloat16).reshape(requests * heads_here, -1),
        flat_values,
        preferred_element_type=jnp.float32,
    ).reshape(requests, heads_here, heads_here, HDIM)
    local_acc = jnp.sum(jnp.where(own_head[None, :, :, None], weighted, 0.0), axis=2)
    stats = jnp.concatenate(
        [local_acc, local_sum[..., None], local_top[..., None]], axis=-1
    )
    stats = butterfly(stats, softmax_merge, reversed(SEQ_PARTS))
    mixture = stats[..., :HDIM]
    totals = stats[..., HDIM]
    top_score = stats[..., HDIM + 1]
    own_score = (
        jnp.einsum("rhd,rhd->rh", queries, new_keys, preferred_element_type=jnp.float32) * 0.125
    )
    final_top = jnp.maximum(top_score, own_score)
    shrink = jnp.exp(top_score - final_top)
    own_expo = jnp.exp(own_score - final_top)
    own_prob = lax.optimization_barrier(own_expo.astype(jnp.bfloat16)).astype(jnp.float32)
    totals = totals * shrink + own_expo
    own_values = new_values.astype(jnp.float32)
    mixture = mixture * shrink[..., None] + own_prob[..., None] * own_values
    mixed = (mixture / totals[..., None]).astype(jnp.bfloat16)
    mixed_rows = mixed.reshape(requests, feat_width)
    out_terms = jnp.dot(mixed_rows, w_out, preferred_element_type=jnp.float32)
    attn_out = butterfly(out_terms, jnp.add, ["heads"]).astype(jnp.bfloat16)
    return (packed_keys, packed_values, packed_request, folded_keys, folded_values, attn_out)


def solution(mesh):
    heads_count, seq_count = mesh.devices.shape
    fine = Mesh(
        mesh.devices.reshape(heads_count, seq_count // 8, 4, 2),
        ("heads",) + SEQ_PARTS,
    )
    seq = SEQ_PARTS
    return jax.shard_map(
        shards,
        mesh=fine,
        in_specs=(
            P(None, seq),
            P(seq, None, "heads"),
            P("heads", seq),
            P(),
            P(),
            P(seq),
            P(seq),
            P(seq, None, "heads"),
            P(seq, None, "heads"),
            P(seq, None),
        ),
        out_specs=(
            P(seq, None, "heads"),
            P(seq, None, "heads"),
            P(seq),
            P(seq, "heads"),
            P(seq, "heads"),
            P(None, seq),
        ),
        check_vma=False,
    )
```

```python
import math

import jax
import jax.numpy as jnp
from jax import lax
from jax.sharding import Mesh
from jax.sharding import PartitionSpec as P

D = 2048
HDIM = 64
ROWS = 128
HOPS = 4
CAP = 4
SLOT_DEV = 16


ROPE_BASE = 130000.0
NORM_EPSILON = 1e-05
MASKED_SCORE = -1e30

SEQ_PARTS = ("z", "x", "core")


AXIS_SIZES = {"heads": 4, "z": 8, "x": 4, "core": 2}


def exchange_steps(axes):
    for axis in axes:
        bit = 1
        while bit < AXIS_SIZES[axis]:
            yield axis, [(i, i ^ bit) for i in range(AXIS_SIZES[axis])]
            bit *= 2


def butterfly(x, merge, axes):
    for axis, pairs in exchange_steps(axes):
        x = merge(x, lax.ppermute(x, axis, pairs))
    return x


def seq_sum(x):
    return butterfly(x, jnp.add, reversed(SEQ_PARTS))


def softmax_merge(mine, theirs):
    top_a, top_b = mine[..., -1:], theirs[..., -1:]
    top = jnp.maximum(top_a, top_b)
    scale_a = jnp.exp(top_a - top)
    scale_b = jnp.exp(top_b - top)
    merged = mine[..., :-1] * scale_a + theirs[..., :-1] * scale_b
    return jnp.concatenate([merged, top], axis=-1)


def seq_index():
    index = lax.axis_index(SEQ_PARTS[0])
    for axis in SEQ_PARTS[1:]:
        index = index * lax.axis_size(axis) + lax.axis_index(axis)
    return index


def seq_size():
    count = 1
    for axis in SEQ_PARTS:
        count *= lax.axis_size(axis)
    return count


def passed_along(array, by):
    count = seq_size()
    return lax.ppermute(array, SEQ_PARTS, [(i, (i + by) % count) for i in range(count)])


def rotate_half(values, cos_table, sin_table):
    half = values.shape[-1] // 2
    lower = values[..., :half]
    upper = values[..., half:]
    return jnp.concatenate(
        [lower * cos_table - upper * sin_table, upper * cos_table + lower * sin_table], axis=-1
    )


def rope_tables(positions, head_size):
    half = head_size // 2
    freqs = ROPE_BASE ** (-(2.0 * jnp.arange(half, dtype=jnp.float32)) / head_size)
    angles = positions.astype(jnp.float32)[:, None] * freqs[None, :]
    return (jnp.cos(angles)[:, None, :], jnp.sin(angles)[:, None, :])


def shards(
    hidden,
    w_qkv,
    w_out,
    positions,
    req_blocks,
    keep_list,
    dest_slot,
    key_cache,
    value_cache,
    fold_weight,
):
    requests = hidden.shape[0]
    n_blocks, row_count, feat_width = key_cache.shape
    heads_here = feat_width // HDIM
    seq_count = seq_size()
    my_index = seq_index()

    widened = hidden.astype(jnp.float32)
    total_sq = seq_sum(jnp.sum(widened * widened, axis=1))
    normed = (widened * lax.rsqrt(total_sq / D + NORM_EPSILON)[:, None]).astype(jnp.bfloat16)
    partial_value = jnp.dot(
        normed, w_qkv.reshape(w_qkv.shape[0], 3 * feat_width), preferred_element_type=jnp.float32
    )
    query_sum = partial_value[:, :feat_width]
    key_values = partial_value[:, feat_width:]
    own_request = jnp.zeros((), jnp.int32)
    for axis, pairs in exchange_steps(reversed(SEQ_PARTS)):
        bit = pairs[0][1]
        upper_half = (lax.axis_index(axis) // bit) % 2 == 1
        half = key_values.shape[0] // 2
        lower, upper = key_values[:half], key_values[half:]
        kept = jnp.where(upper_half, upper, lower)
        given = jnp.where(upper_half, lower, upper)
        payload = jnp.concatenate([query_sum.reshape(-1), given.reshape(-1)])
        payload = lax.ppermute(payload, axis, pairs)
        query_sum = query_sum + payload[: query_sum.size].reshape(query_sum.shape)
        key_values = kept + payload[query_sum.size :].reshape(given.shape)
        own_request = own_request + jnp.where(upper_half, half, 0)
    cos_table, sin_table = rope_tables(positions, HDIM)
    queries = rotate_half(
        query_sum.reshape(requests, heads_here, HDIM), cos_table, sin_table
    ).astype(jnp.bfloat16)
    own_cos = lax.dynamic_index_in_dim(cos_table, own_request, keepdims=True)
    own_sin = lax.dynamic_index_in_dim(sin_table, own_request, keepdims=True)
    own_key = rotate_half(
        key_values[:, :feat_width].reshape(-1, heads_here, HDIM), own_cos[:, 0], own_sin[:, 0]
    ).astype(jnp.bfloat16)
    own_value = key_values[:, feat_width:].reshape(-1, heads_here, HDIM).astype(jnp.bfloat16)

    block_ids = jnp.arange(n_blocks, dtype=jnp.int32)
    global_ids = my_index * n_blocks + block_ids
    req_ends = jnp.cumsum(req_blocks)
    blk_req = jnp.sum((global_ids[:, None] >= req_ends[None, :]).astype(jnp.int32), axis=1)
    is_kept = keep_list == 1

    weight_sum = jnp.sum(fold_weight, axis=1)
    fold_keys = jnp.einsum(
        "bi,bif->bf",
        fold_weight,
        key_cache,
        preferred_element_type=jnp.float32,
        precision=lax.Precision.HIGHEST,
    )
    fold_values = jnp.einsum(
        "bi,bif->bf",
        fold_weight,
        value_cache,
        preferred_element_type=jnp.float32,
        precision=lax.Precision.HIGHEST,
    )
    folded_keys = jnp.where(is_kept[:, None], 0.0, fold_keys / weight_sum[:, None]).astype(
        jnp.bfloat16
    )
    folded_values = jnp.where(is_kept[:, None], 0.0, fold_values / weight_sum[:, None]).astype(
        jnp.bfloat16
    )

    owners = dest_slot // SLOT_DEV
    local_slot = dest_slot % SLOT_DEV
    hop_of = (owners - my_index) % seq_count
    earlier = (
        is_kept[None, :]
        & is_kept[:, None]
        & (hop_of[None, :] == hop_of[:, None])
        & (block_ids[None, :] < block_ids[:, None])
    )
    placed = jnp.sum(earlier.astype(jnp.int32), axis=1)
    arrivals = HOPS * CAP
    send_pos = jnp.where(is_kept, hop_of * CAP + placed, arrivals)
    targets = jnp.arange(arrivals, dtype=jnp.int32)
    hit_table = send_pos[None, :] == targets[:, None]
    has_block = jnp.any(hit_table, axis=1)
    source = jnp.sum(jnp.where(hit_table, block_ids[None, :], 0), axis=1)
    send_keys = key_cache[source].reshape(HOPS, CAP, row_count, feat_width)
    send_values = value_cache[source].reshape(HOPS, CAP, row_count, feat_width)
    meta_data = jnp.stack(
        [jnp.where(has_block, local_slot[source], -1), jnp.where(has_block, blk_req[source], -1)],
        axis=-1,
    )
    meta_data = meta_data.astype(jnp.float32).astype(jnp.bfloat16).reshape(HOPS, CAP, 2)
    arrived = [(send_keys[0], send_values[0], meta_data[0])]
    for distance in range(1, HOPS):
        arrived.append(
            passed_along((send_keys[distance], send_values[distance], meta_data[distance]), distance)
        )
    recv_keys = jnp.stack([entry[0] for entry in arrived])
    recv_values = jnp.stack([entry[1] for entry in arrived])
    recv_meta = jnp.stack([entry[2] for entry in arrived])
    recv_keys = recv_keys.reshape(arrivals, row_count, feat_width)
    recv_values = recv_values.reshape(arrivals, row_count, feat_width)
    recv_meta = recv_meta.reshape(arrivals, 2).astype(jnp.float32).astype(jnp.int32)
    match_table = recv_meta[None, :, 0] == jnp.arange(SLOT_DEV, dtype=jnp.int32)[:, None]
    filled = jnp.any(match_table, axis=1)
    picked = jnp.sum(
        jnp.where(match_table, jnp.arange(arrivals, dtype=jnp.int32)[None, :], 0), axis=1
    )
    packed_keys = jnp.where(filled[:, None, None], recv_keys[picked], jnp.zeros((), jnp.bfloat16))
    packed_values = jnp.where(
        filled[:, None, None], recv_values[picked], jnp.zeros((), jnp.bfloat16)
    )
    packed_request = jnp.where(filled, recv_meta[picked, 1], -1)

    row_keys = key_cache.reshape(-1, heads_here, HDIM)
    row_values = value_cache.reshape(-1, heads_here, HDIM)
    row_req = jnp.repeat(jnp.where(is_kept, blk_req, -1), row_count)
    all_keys = jnp.concatenate(
        [row_keys, folded_keys.reshape(n_blocks, heads_here, HDIM), own_key], axis=0
    )
    all_values = jnp.concatenate(
        [row_values, folded_values.reshape(n_blocks, heads_here, HDIM), own_value], axis=0
    )
    all_req = jnp.concatenate(
        [row_req, jnp.where(is_kept, -1, blk_req), jnp.full((own_key.shape[0],), own_request)]
    )
    bias = jnp.concatenate(
        [
            jnp.zeros((row_req.shape[0],), jnp.float32),
            jnp.full((n_blocks,), math.log(ROWS), jnp.float32),
            jnp.zeros((own_key.shape[0],), jnp.float32),
        ]
    )
    row_mask = all_req[None, :] == jnp.arange(requests, dtype=jnp.int32)[:, None]
    own_head = jnp.arange(heads_here)[:, None] == jnp.arange(heads_here)[None, :]
    spread_queries = jnp.where(
        own_head[None, :, :, None], queries[:, :, None, :], jnp.zeros((), jnp.bfloat16)
    ).reshape(requests * heads_here, feat_width)
    flat_keys = all_keys.reshape(-1, feat_width)
    flat_values = all_values.reshape(-1, feat_width)
    scores = lax.dot_general(
        spread_queries, flat_keys, (((1,), (1,)), ((), ())), preferred_element_type=jnp.float32
    ).reshape(requests, heads_here, -1)
    scores = scores * 0.125 + bias[None, None, :]
    scores = jnp.where(row_mask[:, None, :], scores, MASKED_SCORE)
    local_top = jnp.max(scores, axis=2)
    expo = jnp.where(row_mask[:, None, :], jnp.exp(scores - local_top[..., None]), 0.0)
    local_sum = jnp.sum(expo, axis=2)
    weighted = jnp.dot(
        expo.astype(jnp.bfloat16).reshape(requests * heads_here, -1),
        flat_values,
        preferred_element_type=jnp.float32,
    ).reshape(requests, heads_here, heads_here, HDIM)
    local_acc = jnp.sum(jnp.where(own_head[None, :, :, None], weighted, 0.0), axis=2)
    stats = jnp.concatenate(
        [local_acc, local_sum[..., None], local_top[..., None]], axis=-1
    )
    stats = butterfly(stats, softmax_merge, reversed(SEQ_PARTS))
    mixture = stats[..., :HDIM]
    totals = stats[..., HDIM]
    mixed = (mixture / totals[..., None]).astype(jnp.bfloat16)
    mixed_rows = mixed.reshape(requests, feat_width)
    out_terms = jnp.dot(mixed_rows, w_out, preferred_element_type=jnp.float32)
    attn_out = butterfly(out_terms, jnp.add, ["heads"]).astype(jnp.bfloat16)
    return (packed_keys, packed_values, packed_request, folded_keys, folded_values, attn_out)


def solution(mesh):
    heads_count, seq_count = mesh.devices.shape
    fine = Mesh(
        mesh.devices.reshape(heads_count, seq_count // 8, 4, 2),
        ("heads",) + SEQ_PARTS,
    )
    seq = SEQ_PARTS
    return jax.shard_map(
        shards,
        mesh=fine,
        in_specs=(
            P(None, seq),
            P(seq, None, "heads"),
            P("heads", seq),
            P(),
            P(),
            P(seq),
            P(seq),
            P(seq, None, "heads"),
            P(seq, None, "heads"),
            P(seq, None),
        ),
        out_specs=(
            P(seq, None, "heads"),
            P(seq, None, "heads"),
            P(seq),
            P(seq, "heads"),
            P(seq, "heads"),
            P(None, seq),
        ),
        check_vma=False,
    )
```

```python
import math

import jax
import jax.numpy as jnp
from jax import lax
from jax.sharding import Mesh
from jax.sharding import PartitionSpec as P

D = 2048
HDIM = 64
ROWS = 128
HOPS = 4
CAP = 4
SLOT_DEV = 16


ROPE_BASE = 130000.0
NORM_EPSILON = 1e-05
MASKED_SCORE = -1e30

SEQ_PARTS = ("z", "x", "core")


AXIS_SIZES = {"heads": 4, "z": 8, "x": 4, "core": 2}


def exchange_steps(axes):
    for axis in axes:
        bit = 1
        while bit < AXIS_SIZES[axis]:
            yield axis, [(i, i ^ bit) for i in range(AXIS_SIZES[axis])]
            bit *= 2


def butterfly(x, merge, axes):
    for axis, pairs in exchange_steps(axes):
        x = merge(x, lax.ppermute(x, axis, pairs))
    return x


def seq_sum(x):
    return butterfly(x, jnp.add, reversed(SEQ_PARTS))


def softmax_merge(mine, theirs):
    top_a, top_b = mine[..., -1:], theirs[..., -1:]
    top = jnp.maximum(top_a, top_b)
    scale_a = jnp.exp(top_a - top)
    scale_b = jnp.exp(top_b - top)
    merged = mine[..., :-1] * scale_a + theirs[..., :-1] * scale_b
    return jnp.concatenate([merged, top], axis=-1)


def seq_index():
    index = lax.axis_index(SEQ_PARTS[0])
    for axis in SEQ_PARTS[1:]:
        index = index * lax.axis_size(axis) + lax.axis_index(axis)
    return index


def seq_size():
    count = 1
    for axis in SEQ_PARTS:
        count *= lax.axis_size(axis)
    return count


def passed_along(array, by):
    count = seq_size()
    return lax.ppermute(array, SEQ_PARTS, [(i, (i + by) % count) for i in range(count)])


def rotate_half(values, cos_table, sin_table):
    half = values.shape[-1] // 2
    lower = values[..., :half]
    upper = values[..., half:]
    return jnp.concatenate(
        [lower * cos_table - upper * sin_table, upper * cos_table + lower * sin_table], axis=-1
    )


def rope_tables(positions, head_size):
    half = head_size // 2
    freqs = ROPE_BASE ** (-(2.0 * jnp.arange(half, dtype=jnp.float32)) / head_size)
    angles = positions.astype(jnp.float32)[:, None] * freqs[None, :]
    return (jnp.cos(angles)[:, None, :], jnp.sin(angles)[:, None, :])


def shards(
    hidden,
    w_qkv,
    w_out,
    positions,
    req_blocks,
    keep_list,
    dest_slot,
    key_cache,
    value_cache,
    fold_weight,
):
    requests = hidden.shape[0]
    n_blocks, row_count, feat_width = key_cache.shape
    heads_here = feat_width // HDIM
    seq_count = seq_size()
    my_index = seq_index()

    widened = hidden.astype(jnp.float32)
    total_sq = seq_sum(jnp.sum(widened * widened, axis=1))
    normed = (widened * lax.rsqrt(total_sq / D + NORM_EPSILON)[:, None]).astype(jnp.bfloat16)
    partial_value = jnp.dot(
        normed, w_qkv.reshape(w_qkv.shape[0], 3 * feat_width), preferred_element_type=jnp.float32
    )
    query_sum = partial_value[:, :feat_width]
    key_values = partial_value[:, feat_width:]
    own_request = jnp.zeros((), jnp.int32)
    for axis, pairs in exchange_steps(reversed(SEQ_PARTS)):
        bit = pairs[0][1]
        upper_half = (lax.axis_index(axis) // bit) % 2 == 1
        half = key_values.shape[0] // 2
        lower, upper = key_values[:half], key_values[half:]
        kept = jnp.where(upper_half, upper, lower)
        given = jnp.where(upper_half, lower, upper)
        payload = jnp.concatenate([query_sum.reshape(-1), given.reshape(-1)])
        payload = lax.ppermute(payload, axis, pairs)
        query_sum = query_sum + payload[: query_sum.size].reshape(query_sum.shape)
        key_values = kept + payload[query_sum.size :].reshape(given.shape)
        own_request = own_request + jnp.where(upper_half, half, 0)
    cos_table, sin_table = rope_tables(positions, HDIM)
    queries = rotate_half(
        query_sum.reshape(requests, heads_here, HDIM), cos_table, sin_table
    ).astype(jnp.bfloat16)
    own_cos = lax.dynamic_index_in_dim(cos_table, own_request, keepdims=True)
    own_sin = lax.dynamic_index_in_dim(sin_table, own_request, keepdims=True)
    own_key = rotate_half(
        key_values[:, :feat_width].reshape(-1, heads_here, HDIM), own_cos[:, 0], own_sin[:, 0]
    ).astype(jnp.bfloat16)
    own_value = key_values[:, feat_width:].reshape(-1, heads_here, HDIM).astype(jnp.bfloat16)

    block_ids = jnp.arange(n_blocks, dtype=jnp.int32)
    global_ids = my_index * n_blocks + block_ids
    req_ends = jnp.cumsum(req_blocks)
    blk_req = jnp.sum((global_ids[:, None] >= req_ends[None, :]).astype(jnp.int32), axis=1)
    is_kept = keep_list == 1

    weight_sum = jnp.sum(fold_weight, axis=1)
    fold_keys = jnp.einsum(
        "bi,bif->bf",
        fold_weight,
        key_cache,
        preferred_element_type=jnp.float32,
        precision=lax.Precision.HIGHEST,
    )
    fold_values = jnp.einsum(
        "bi,bif->bf",
        fold_weight,
        value_cache,
        preferred_element_type=jnp.float32,
        precision=lax.Precision.HIGHEST,
    )
    folded_keys = jnp.where(is_kept[:, None], 0.0, fold_keys / weight_sum[:, None]).astype(
        jnp.bfloat16
    )
    folded_values = jnp.where(is_kept[:, None], 0.0, fold_values / weight_sum[:, None]).astype(
        jnp.bfloat16
    )

    owners = dest_slot // SLOT_DEV
    local_slot = dest_slot % SLOT_DEV
    hop_of = (owners - my_index) % seq_count
    earlier = (
        is_kept[None, :]
        & is_kept[:, None]
        & (hop_of[None, :] == hop_of[:, None])
        & (block_ids[None, :] < block_ids[:, None])
    )
    placed = jnp.sum(earlier.astype(jnp.int32), axis=1)
    arrivals = HOPS * CAP
    send_pos = jnp.where(is_kept, hop_of * CAP + placed, arrivals)
    targets = jnp.arange(arrivals, dtype=jnp.int32)
    hit_table = send_pos[None, :] == targets[:, None]
    has_block = jnp.any(hit_table, axis=1)
    source = jnp.sum(jnp.where(hit_table, block_ids[None, :], 0), axis=1)
    send_keys = key_cache[source].reshape(HOPS, CAP, row_count, feat_width)
    send_values = value_cache[source].reshape(HOPS, CAP, row_count, feat_width)
    meta_data = jnp.stack(
        [jnp.where(has_block, local_slot[source], -1), jnp.where(has_block, blk_req[source], -1)],
        axis=-1,
    )
    meta_data = meta_data.astype(jnp.float32).astype(jnp.bfloat16).reshape(HOPS, CAP, 2)
    arrived = [(send_keys[0], send_values[0], meta_data[0])]
    for distance in range(1, HOPS):
        arrived.append(
            passed_along((send_keys[distance], send_values[distance], meta_data[distance]), distance)
        )
    recv_keys = jnp.stack([entry[0] for entry in arrived])
    recv_values = jnp.stack([entry[1] for entry in arrived])
    recv_meta = jnp.stack([entry[2] for entry in arrived])
    recv_keys = recv_keys.reshape(arrivals, row_count, feat_width)
    recv_values = recv_values.reshape(arrivals, row_count, feat_width)
    recv_meta = recv_meta.reshape(arrivals, 2).astype(jnp.float32).astype(jnp.int32)
    match_table = recv_meta[None, :, 0] == jnp.arange(SLOT_DEV, dtype=jnp.int32)[:, None]
    filled = jnp.any(match_table, axis=1)
    picked = jnp.sum(
        jnp.where(match_table, jnp.arange(arrivals, dtype=jnp.int32)[None, :], 0), axis=1
    )
    packed_keys = jnp.where(filled[:, None, None], recv_keys[picked], jnp.zeros((), jnp.bfloat16))
    packed_values = jnp.where(
        filled[:, None, None], recv_values[picked], jnp.zeros((), jnp.bfloat16)
    )
    packed_request = jnp.where(filled, recv_meta[picked, 1], -1)

    row_req = jnp.repeat(jnp.where(is_kept, blk_req, -1), row_count)
    extra_keys = jnp.concatenate([folded_keys, own_key.reshape(-1, feat_width)], axis=0)
    extra_values = jnp.concatenate([folded_values, own_value.reshape(-1, feat_width)], axis=0)
    extra_req = jnp.concatenate(
        [jnp.where(is_kept, -1, blk_req), jnp.full((own_key.shape[0],), own_request)]
    )
    extra_bias = jnp.concatenate(
        [
            jnp.full((n_blocks,), math.log(ROWS), jnp.float32),
            jnp.zeros((own_key.shape[0],), jnp.float32),
        ]
    )
    request_ids = jnp.arange(requests, dtype=jnp.int32)[:, None]
    row_mask = (row_req[None, :] == request_ids)[:, None, :]
    extra_mask = (extra_req[None, :] == request_ids)[:, None, :]
    own_head = jnp.arange(heads_here)[:, None] == jnp.arange(heads_here)[None, :]
    spread_queries = jnp.where(
        own_head[None, :, :, None], queries[:, :, None, :], jnp.zeros((), jnp.bfloat16)
    ).reshape(requests * heads_here, feat_width)

    def scores_of(keys, mask, bias):
        raw = lax.dot_general(
            spread_queries, keys, (((1,), (1,)), ((), ())), preferred_element_type=jnp.float32
        ).reshape(requests, heads_here, -1)
        return jnp.where(mask, raw * 0.125 + bias, MASKED_SCORE)

    row_scores = scores_of(key_cache.reshape(-1, feat_width), row_mask, 0.0)
    extra_scores = scores_of(extra_keys, extra_mask, extra_bias[None, None, :])
    local_top = jnp.maximum(jnp.max(row_scores, axis=2), jnp.max(extra_scores, axis=2))
    row_expo = jnp.where(row_mask, jnp.exp(row_scores - local_top[..., None]), 0.0)
    extra_expo = jnp.where(extra_mask, jnp.exp(extra_scores - local_top[..., None]), 0.0)
    local_sum = jnp.sum(row_expo, axis=2) + jnp.sum(extra_expo, axis=2)

    def weighted_of(expo, values):
        return jnp.dot(
            expo.astype(jnp.bfloat16).reshape(requests * heads_here, -1),
            values,
            preferred_element_type=jnp.float32,
        )

    weighted = weighted_of(row_expo, value_cache.reshape(-1, feat_width)) + weighted_of(
        extra_expo, extra_values
    )
    weighted = weighted.reshape(requests, heads_here, heads_here, HDIM)
    local_acc = jnp.sum(jnp.where(own_head[None, :, :, None], weighted, 0.0), axis=2)
    stats = jnp.concatenate(
        [local_acc, local_sum[..., None], local_top[..., None]], axis=-1
    )
    stats = butterfly(stats, softmax_merge, reversed(SEQ_PARTS))
    mixture = stats[..., :HDIM]
    totals = stats[..., HDIM]
    mixed = (mixture / totals[..., None]).astype(jnp.bfloat16)
    mixed_rows = mixed.reshape(requests, feat_width)
    out_terms = jnp.dot(mixed_rows, w_out, preferred_element_type=jnp.float32)
    attn_out = butterfly(out_terms, jnp.add, ["heads"]).astype(jnp.bfloat16)
    return (packed_keys, packed_values, packed_request, folded_keys, folded_values, attn_out)


def solution(mesh):
    heads_count, seq_count = mesh.devices.shape
    fine = Mesh(
        mesh.devices.reshape(heads_count, seq_count // 8, 4, 2),
        ("heads",) + SEQ_PARTS,
    )
    seq = SEQ_PARTS
    return jax.shard_map(
        shards,
        mesh=fine,
        in_specs=(
            P(None, seq),
            P(seq, None, "heads"),
            P("heads", seq),
            P(),
            P(),
            P(seq),
            P(seq),
            P(seq, None, "heads"),
            P(seq, None, "heads"),
            P(seq, None),
        ),
        out_specs=(
            P(seq, None, "heads"),
            P(seq, None, "heads"),
            P(seq),
            P(seq, "heads"),
            P(seq, "heads"),
            P(None, seq),
        ),
        check_vma=False,
    )
```

```python
import math

import jax
import jax.numpy as jnp
from jax import lax
from jax.sharding import Mesh
from jax.sharding import PartitionSpec as P

D = 2048
HDIM = 64
ROWS = 128
HOPS = 4
CAP = 4
SLOT_DEV = 16


ROPE_BASE = 130000.0
NORM_EPSILON = 1e-05
MASKED_SCORE = -1e30

SEQ_PARTS = ("z", "x", "core")


AXIS_SIZES = {"heads": 4, "z": 8, "x": 4, "core": 2}


def exchange_steps(axes):
    for axis in axes:
        bit = 1
        while bit < AXIS_SIZES[axis]:
            yield axis, [(i, i ^ bit) for i in range(AXIS_SIZES[axis])]
            bit *= 2


def butterfly(x, merge, axes):
    for axis, pairs in exchange_steps(axes):
        x = merge(x, lax.ppermute(x, axis, pairs))
    return x


def seq_sum(x):
    return butterfly(x, jnp.add, reversed(SEQ_PARTS))


def softmax_merge(mine, theirs):
    top_a, top_b = mine[..., -1:], theirs[..., -1:]
    top = jnp.maximum(top_a, top_b)
    scale_a = jnp.exp(top_a - top)
    scale_b = jnp.exp(top_b - top)
    merged = mine[..., :-1] * scale_a + theirs[..., :-1] * scale_b
    return jnp.concatenate([merged, top], axis=-1)


def seq_index():
    index = lax.axis_index(SEQ_PARTS[0])
    for axis in SEQ_PARTS[1:]:
        index = index * lax.axis_size(axis) + lax.axis_index(axis)
    return index


def seq_size():
    count = 1
    for axis in SEQ_PARTS:
        count *= lax.axis_size(axis)
    return count


def passed_along(array, by):
    count = seq_size()
    return lax.ppermute(array, SEQ_PARTS, [(i, (i + by) % count) for i in range(count)])


def rotate_half(values, cos_table, sin_table):
    half = values.shape[-1] // 2
    lower = values[..., :half]
    upper = values[..., half:]
    return jnp.concatenate(
        [lower * cos_table - upper * sin_table, upper * cos_table + lower * sin_table], axis=-1
    )


def rope_tables(positions, head_size):
    half = head_size // 2
    freqs = ROPE_BASE ** (-(2.0 * jnp.arange(half, dtype=jnp.float32)) / head_size)
    angles = positions.astype(jnp.float32)[:, None] * freqs[None, :]
    return (jnp.cos(angles)[:, None, :], jnp.sin(angles)[:, None, :])


def shards(
    hidden,
    w_qkv,
    w_out,
    positions,
    req_blocks,
    keep_list,
    dest_slot,
    key_cache,
    value_cache,
    fold_weight,
):
    requests = hidden.shape[0]
    n_blocks, row_count, feat_width = key_cache.shape
    heads_here = feat_width // HDIM
    seq_count = seq_size()
    my_index = seq_index()

    widened = hidden.astype(jnp.float32)
    total_sq = seq_sum(jnp.sum(widened * widened, axis=1))
    normed = (widened * lax.rsqrt(total_sq / D + NORM_EPSILON)[:, None]).astype(jnp.bfloat16)
    partial_value = jnp.dot(
        normed, w_qkv.reshape(w_qkv.shape[0], 3 * feat_width), preferred_element_type=jnp.float32
    )
    query_sum = partial_value[:, :feat_width]
    key_values = partial_value[:, feat_width:]
    own_request = jnp.zeros((), jnp.int32)
    for axis, pairs in exchange_steps(reversed(SEQ_PARTS)):
        bit = pairs[0][1]
        upper_half = (lax.axis_index(axis) // bit) % 2 == 1
        half = key_values.shape[0] // 2
        lower, upper = key_values[:half], key_values[half:]
        kept = jnp.where(upper_half, upper, lower)
        given = jnp.where(upper_half, lower, upper)
        payload = jnp.concatenate([query_sum.reshape(-1), given.reshape(-1)])
        payload = lax.ppermute(payload, axis, pairs)
        query_sum = query_sum + payload[: query_sum.size].reshape(query_sum.shape)
        key_values = kept + payload[query_sum.size :].reshape(given.shape)
        own_request = own_request + jnp.where(upper_half, half, 0)
    cos_table, sin_table = rope_tables(positions, HDIM)
    queries = rotate_half(
        query_sum.reshape(requests, heads_here, HDIM), cos_table, sin_table
    ).astype(jnp.bfloat16)
    own_cos = lax.dynamic_index_in_dim(cos_table, own_request, keepdims=True)
    own_sin = lax.dynamic_index_in_dim(sin_table, own_request, keepdims=True)
    own_key = rotate_half(
        key_values[:, :feat_width].reshape(-1, heads_here, HDIM), own_cos[:, 0], own_sin[:, 0]
    ).astype(jnp.bfloat16)
    own_value = key_values[:, feat_width:].reshape(-1, heads_here, HDIM).astype(jnp.bfloat16)

    block_ids = jnp.arange(n_blocks, dtype=jnp.int32)
    global_ids = my_index * n_blocks + block_ids
    req_ends = jnp.cumsum(req_blocks)
    blk_req = jnp.sum((global_ids[:, None] >= req_ends[None, :]).astype(jnp.int32), axis=1)
    is_kept = keep_list == 1

    weight_sum = jnp.sum(fold_weight, axis=1)
    fold_keys = jnp.einsum(
        "bi,bif->bf",
        fold_weight,
        key_cache,
        preferred_element_type=jnp.float32,
        precision=lax.Precision.HIGHEST,
    )
    fold_values = jnp.einsum(
        "bi,bif->bf",
        fold_weight,
        value_cache,
        preferred_element_type=jnp.float32,
        precision=lax.Precision.HIGHEST,
    )
    folded_keys = jnp.where(is_kept[:, None], 0.0, fold_keys / weight_sum[:, None]).astype(
        jnp.bfloat16
    )
    folded_values = jnp.where(is_kept[:, None], 0.0, fold_values / weight_sum[:, None]).astype(
        jnp.bfloat16
    )

    owners = dest_slot // SLOT_DEV
    local_slot = dest_slot % SLOT_DEV
    hop_of = (owners - my_index) % seq_count
    earlier = (
        is_kept[None, :]
        & is_kept[:, None]
        & (hop_of[None, :] == hop_of[:, None])
        & (block_ids[None, :] < block_ids[:, None])
    )
    placed = jnp.sum(earlier.astype(jnp.int32), axis=1)
    arrivals = HOPS * CAP
    send_pos = jnp.where(is_kept, hop_of * CAP + placed, arrivals)
    targets = jnp.arange(arrivals, dtype=jnp.int32)
    hit_table = send_pos[None, :] == targets[:, None]
    has_block = jnp.any(hit_table, axis=1)
    source = jnp.sum(jnp.where(hit_table, block_ids[None, :], 0), axis=1)
    send_keys = key_cache[source].reshape(HOPS, CAP, row_count, feat_width)
    send_values = value_cache[source].reshape(HOPS, CAP, row_count, feat_width)
    meta_data = jnp.stack(
        [jnp.where(has_block, local_slot[source], -1), jnp.where(has_block, blk_req[source], -1)],
        axis=-1,
    )
    meta_data = meta_data.astype(jnp.float32).astype(jnp.bfloat16).reshape(HOPS, CAP, 2)
    arrived = [(send_keys[0], send_values[0], meta_data[0])]
    for distance in range(1, HOPS):
        arrived.append(
            passed_along((send_keys[distance], send_values[distance], meta_data[distance]), distance)
        )
    recv_keys = jnp.stack([entry[0] for entry in arrived])
    recv_values = jnp.stack([entry[1] for entry in arrived])
    recv_meta = jnp.stack([entry[2] for entry in arrived])
    recv_keys = recv_keys.reshape(arrivals, row_count, feat_width)
    recv_values = recv_values.reshape(arrivals, row_count, feat_width)
    recv_meta = recv_meta.reshape(arrivals, 2).astype(jnp.float32).astype(jnp.int32)
    match_table = recv_meta[None, :, 0] == jnp.arange(SLOT_DEV, dtype=jnp.int32)[:, None]
    filled = jnp.any(match_table, axis=1)
    picked = jnp.sum(
        jnp.where(match_table, jnp.arange(arrivals, dtype=jnp.int32)[None, :], 0), axis=1
    )
    packed_keys = jnp.where(filled[:, None, None], recv_keys[picked], jnp.zeros((), jnp.bfloat16))
    packed_values = jnp.where(
        filled[:, None, None], recv_values[picked], jnp.zeros((), jnp.bfloat16)
    )
    packed_request = jnp.where(filled, recv_meta[picked, 1], -1)

    row_req = jnp.repeat(jnp.where(is_kept, blk_req, -1), row_count)
    extra_keys = jnp.concatenate([folded_keys, own_key.reshape(-1, feat_width)], axis=0)
    extra_values = jnp.concatenate([folded_values, own_value.reshape(-1, feat_width)], axis=0)
    extra_req = jnp.concatenate(
        [jnp.where(is_kept, -1, blk_req), jnp.full((own_key.shape[0],), own_request)]
    )
    extra_bias = jnp.concatenate(
        [
            jnp.full((n_blocks,), math.log(ROWS), jnp.float32),
            jnp.zeros((own_key.shape[0],), jnp.float32),
        ]
    )
    request_ids = jnp.arange(requests, dtype=jnp.int32)[:, None]
    row_mask = (row_req[None, :] == request_ids)[:, None, :]
    extra_mask = (extra_req[None, :] == request_ids)[:, None, :]
    own_head = jnp.arange(heads_here)[:, None] == jnp.arange(heads_here)[None, :]
    spread_queries = jnp.where(
        own_head[None, :, :, None], queries[:, :, None, :], jnp.zeros((), jnp.bfloat16)
    ).reshape(requests * heads_here, feat_width)

    def scores_of(keys, mask, bias):
        raw = lax.dot_general(
            spread_queries, keys, (((1,), (1,)), ((), ())), preferred_element_type=jnp.float32
        ).reshape(requests, heads_here, -1)
        return jnp.where(mask, raw * 0.125 + bias, MASKED_SCORE)

    row_scores = scores_of(key_cache.reshape(-1, feat_width), row_mask, 0.0)
    extra_scores = scores_of(extra_keys, extra_mask, extra_bias[None, None, :])
    local_top = jnp.maximum(jnp.max(row_scores, axis=2), jnp.max(extra_scores, axis=2))
    row_expo = jnp.where(row_mask, jnp.exp(row_scores - local_top[..., None]), 0.0)
    extra_expo = jnp.where(extra_mask, jnp.exp(extra_scores - local_top[..., None]), 0.0)
    local_sum = jnp.sum(row_expo, axis=2) + jnp.sum(extra_expo, axis=2)

    def weighted_of(expo, values):
        return jnp.dot(
            expo.astype(jnp.bfloat16).reshape(requests * heads_here, -1),
            values,
            preferred_element_type=jnp.float32,
        )

    weighted = weighted_of(row_expo, value_cache.reshape(-1, feat_width)) + weighted_of(
        extra_expo, extra_values
    )
    weighted = weighted.reshape(requests, heads_here, heads_here, HDIM)
    local_acc = jnp.sum(jnp.where(own_head[None, :, :, None], weighted, 0.0), axis=2)
    stats = jnp.concatenate(
        [local_acc, local_sum[..., None], local_top[..., None]], axis=-1
    )
    stats = butterfly(stats, softmax_merge, ["z", "core", "x"])
    mixture = stats[..., :HDIM]
    totals = stats[..., HDIM]
    mixed = (mixture / totals[..., None]).astype(jnp.bfloat16)
    mixed_rows = mixed.reshape(requests, feat_width)
    out_terms = jnp.dot(mixed_rows, w_out, preferred_element_type=jnp.float32)
    attn_out = butterfly(out_terms, jnp.add, ["heads"]).astype(jnp.bfloat16)
    return (packed_keys, packed_values, packed_request, folded_keys, folded_values, attn_out)


def solution(mesh):
    heads_count, seq_count = mesh.devices.shape
    fine = Mesh(
        mesh.devices.reshape(heads_count, seq_count // 8, 4, 2),
        ("heads",) + SEQ_PARTS,
    )
    seq = SEQ_PARTS
    return jax.shard_map(
        shards,
        mesh=fine,
        in_specs=(
            P(None, seq),
            P(seq, None, "heads"),
            P("heads", seq),
            P(),
            P(),
            P(seq),
            P(seq),
            P(seq, None, "heads"),
            P(seq, None, "heads"),
            P(seq, None),
        ),
        out_specs=(
            P(seq, None, "heads"),
            P(seq, None, "heads"),
            P(seq),
            P(seq, "heads"),
            P(seq, "heads"),
            P(None, seq),
        ),
        check_vma=False,
    )
```

```python
import math

import jax
import jax.numpy as jnp
from jax import lax
from jax.sharding import Mesh
from jax.sharding import PartitionSpec as P

D = 2048
HDIM = 64
ROWS = 128
HOPS = 4
CAP = 4
SLOT_DEV = 16


ROPE_BASE = 130000.0
NORM_EPSILON = 1e-05
MASKED_SCORE = -1e30

SEQ_PARTS = ("z", "x", "core")


AXIS_SIZES = {"heads": 4, "z": 8, "x": 4, "core": 2}


def exchange_steps(axes):
    for axis in axes:
        bit = 1
        while bit < AXIS_SIZES[axis]:
            yield axis, [(i, i ^ bit) for i in range(AXIS_SIZES[axis])]
            bit *= 2


def butterfly(x, merge, axes):
    for axis, pairs in exchange_steps(axes):
        x = merge(x, lax.ppermute(x, axis, pairs))
    return x


def seq_sum(x):
    return butterfly(x, jnp.add, reversed(SEQ_PARTS))


def softmax_merge(mine, theirs):
    top_a, top_b = mine[..., -1:], theirs[..., -1:]
    top = jnp.maximum(top_a, top_b)
    scale_a = jnp.exp(top_a - top)
    scale_b = jnp.exp(top_b - top)
    merged = mine[..., :-1] * scale_a + theirs[..., :-1] * scale_b
    return jnp.concatenate([merged, top], axis=-1)


def seq_index():
    index = lax.axis_index(SEQ_PARTS[0])
    for axis in SEQ_PARTS[1:]:
        index = index * lax.axis_size(axis) + lax.axis_index(axis)
    return index


def seq_size():
    count = 1
    for axis in SEQ_PARTS:
        count *= lax.axis_size(axis)
    return count


def passed_along(array, by):
    count = seq_size()
    return lax.ppermute(array, SEQ_PARTS, [(i, (i + by) % count) for i in range(count)])


def rotate_half(values, cos_table, sin_table):
    half = values.shape[-1] // 2
    lower = values[..., :half]
    upper = values[..., half:]
    return jnp.concatenate(
        [lower * cos_table - upper * sin_table, upper * cos_table + lower * sin_table], axis=-1
    )


def rope_tables(positions, head_size):
    half = head_size // 2
    freqs = ROPE_BASE ** (-(2.0 * jnp.arange(half, dtype=jnp.float32)) / head_size)
    angles = positions.astype(jnp.float32)[:, None] * freqs[None, :]
    return (jnp.cos(angles)[:, None, :], jnp.sin(angles)[:, None, :])


def shards(
    hidden,
    w_qkv,
    w_out,
    positions,
    req_blocks,
    keep_list,
    dest_slot,
    key_cache,
    value_cache,
    fold_weight,
):
    requests = hidden.shape[0]
    n_blocks, row_count, feat_width = key_cache.shape
    heads_here = feat_width // HDIM
    seq_count = seq_size()
    my_index = seq_index()

    widened = hidden.astype(jnp.float32)
    total_sq = seq_sum(jnp.sum(widened * widened, axis=1))
    normed = (widened * lax.rsqrt(total_sq / D + NORM_EPSILON)[:, None]).astype(jnp.bfloat16)
    partial_value = jnp.dot(
        normed, w_qkv.reshape(w_qkv.shape[0], 3 * feat_width), preferred_element_type=jnp.float32
    )
    query_sum = partial_value[:, :feat_width]
    key_values = partial_value[:, feat_width:]
    own_request = jnp.zeros((), jnp.int32)
    for axis, pairs in exchange_steps(reversed(SEQ_PARTS)):
        bit = pairs[0][1]
        upper_half = (lax.axis_index(axis) // bit) % 2 == 1
        half = key_values.shape[0] // 2
        lower, upper = key_values[:half], key_values[half:]
        kept = jnp.where(upper_half, upper, lower)
        given = jnp.where(upper_half, lower, upper)
        payload = jnp.concatenate([query_sum.reshape(-1), given.reshape(-1)])
        payload = lax.ppermute(payload, axis, pairs)
        query_sum = query_sum + payload[: query_sum.size].reshape(query_sum.shape)
        key_values = kept + payload[query_sum.size :].reshape(given.shape)
        own_request = own_request + jnp.where(upper_half, half, 0)
    cos_table, sin_table = rope_tables(positions, HDIM)
    queries = rotate_half(
        query_sum.reshape(requests, heads_here, HDIM), cos_table, sin_table
    ).astype(jnp.bfloat16)
    own_cos = lax.dynamic_index_in_dim(cos_table, own_request, keepdims=True)
    own_sin = lax.dynamic_index_in_dim(sin_table, own_request, keepdims=True)
    own_key = rotate_half(
        key_values[:, :feat_width].reshape(-1, heads_here, HDIM), own_cos[:, 0], own_sin[:, 0]
    ).astype(jnp.bfloat16)
    own_value = key_values[:, feat_width:].reshape(-1, heads_here, HDIM).astype(jnp.bfloat16)

    block_ids = jnp.arange(n_blocks, dtype=jnp.int32)
    global_ids = my_index * n_blocks + block_ids
    req_ends = jnp.cumsum(req_blocks)
    blk_req = jnp.sum((global_ids[:, None] >= req_ends[None, :]).astype(jnp.int32), axis=1)
    is_kept = keep_list == 1

    weight_sum = jnp.sum(fold_weight, axis=1)
    fold_keys = jnp.einsum(
        "bi,bif->bf",
        fold_weight,
        key_cache,
        preferred_element_type=jnp.float32,
        precision=lax.Precision.HIGHEST,
    )
    fold_values = jnp.einsum(
        "bi,bif->bf",
        fold_weight,
        value_cache,
        preferred_element_type=jnp.float32,
        precision=lax.Precision.HIGHEST,
    )
    folded_keys = jnp.where(is_kept[:, None], 0.0, fold_keys / weight_sum[:, None]).astype(
        jnp.bfloat16
    )
    folded_values = jnp.where(is_kept[:, None], 0.0, fold_values / weight_sum[:, None]).astype(
        jnp.bfloat16
    )

    owners = dest_slot // SLOT_DEV
    local_slot = dest_slot % SLOT_DEV
    hop_of = (owners - my_index) % seq_count
    earlier = (
        is_kept[None, :]
        & is_kept[:, None]
        & (hop_of[None, :] == hop_of[:, None])
        & (block_ids[None, :] < block_ids[:, None])
    )
    placed = jnp.sum(earlier.astype(jnp.int32), axis=1)
    arrivals = HOPS * CAP
    send_pos = jnp.where(is_kept, hop_of * CAP + placed, arrivals)
    targets = jnp.arange(arrivals, dtype=jnp.int32)
    hit_table = send_pos[None, :] == targets[:, None]
    has_block = jnp.any(hit_table, axis=1)
    source = jnp.sum(jnp.where(hit_table, block_ids[None, :], 0), axis=1)
    send_blocks = jnp.stack([key_cache[source], value_cache[source]], axis=1).reshape(
        HOPS, CAP, 2, row_count, feat_width
    )
    meta_data = jnp.stack(
        [jnp.where(has_block, local_slot[source], -1), jnp.where(has_block, blk_req[source], -1)],
        axis=-1,
    )
    meta_data = meta_data.astype(jnp.float32).astype(jnp.bfloat16).reshape(HOPS, CAP, 2)
    arrived = [(send_blocks[0], meta_data[0])]
    for distance in range(1, HOPS):
        arrived.append(passed_along((send_blocks[distance], meta_data[distance]), distance))
    recv_blocks = jnp.stack([entry[0] for entry in arrived])
    recv_meta = jnp.stack([entry[1] for entry in arrived])
    recv_blocks = recv_blocks.reshape(arrivals, 2, row_count, feat_width)
    recv_meta = recv_meta.reshape(arrivals, 2).astype(jnp.float32).astype(jnp.int32)
    match_table = recv_meta[None, :, 0] == jnp.arange(SLOT_DEV, dtype=jnp.int32)[:, None]
    filled = jnp.any(match_table, axis=1)
    picked = jnp.sum(
        jnp.where(match_table, jnp.arange(arrivals, dtype=jnp.int32)[None, :], 0), axis=1
    )
    packed_blocks = jnp.where(
        filled[:, None, None, None], recv_blocks[picked], jnp.zeros((), jnp.bfloat16)
    )
    packed_keys = packed_blocks[:, 0]
    packed_values = packed_blocks[:, 1]
    packed_request = jnp.where(filled, recv_meta[picked, 1], -1)

    row_req = jnp.repeat(jnp.where(is_kept, blk_req, -1), row_count)
    extra_keys = jnp.concatenate([folded_keys, own_key.reshape(-1, feat_width)], axis=0)
    extra_values = jnp.concatenate([folded_values, own_value.reshape(-1, feat_width)], axis=0)
    extra_req = jnp.concatenate(
        [jnp.where(is_kept, -1, blk_req), jnp.full((own_key.shape[0],), own_request)]
    )
    extra_bias = jnp.concatenate(
        [
            jnp.full((n_blocks,), math.log(ROWS), jnp.float32),
            jnp.zeros((own_key.shape[0],), jnp.float32),
        ]
    )
    request_ids = jnp.arange(requests, dtype=jnp.int32)[:, None]
    row_mask = (row_req[None, :] == request_ids)[:, None, :]
    extra_mask = (extra_req[None, :] == request_ids)[:, None, :]
    own_head = jnp.arange(heads_here)[:, None] == jnp.arange(heads_here)[None, :]
    spread_queries = jnp.where(
        own_head[None, :, :, None], queries[:, :, None, :], jnp.zeros((), jnp.bfloat16)
    ).reshape(requests * heads_here, feat_width)

    def scores_of(keys, mask, bias):
        raw = lax.dot_general(
            spread_queries, keys, (((1,), (1,)), ((), ())), preferred_element_type=jnp.float32
        ).reshape(requests, heads_here, -1)
        return jnp.where(mask, raw * 0.125 + bias, MASKED_SCORE)

    row_scores = scores_of(key_cache.reshape(-1, feat_width), row_mask, 0.0)
    extra_scores = scores_of(extra_keys, extra_mask, extra_bias[None, None, :])
    local_top = jnp.maximum(jnp.max(row_scores, axis=2), jnp.max(extra_scores, axis=2))
    row_expo = jnp.where(row_mask, jnp.exp(row_scores - local_top[..., None]), 0.0)
    extra_expo = jnp.where(extra_mask, jnp.exp(extra_scores - local_top[..., None]), 0.0)
    local_sum = jnp.sum(row_expo, axis=2) + jnp.sum(extra_expo, axis=2)

    def weighted_of(expo, values):
        return jnp.dot(
            expo.astype(jnp.bfloat16).reshape(requests * heads_here, -1),
            values,
            preferred_element_type=jnp.float32,
        )

    weighted = weighted_of(row_expo, value_cache.reshape(-1, feat_width)) + weighted_of(
        extra_expo, extra_values
    )
    weighted = weighted.reshape(requests, heads_here, heads_here, HDIM)
    local_acc = jnp.sum(jnp.where(own_head[None, :, :, None], weighted, 0.0), axis=2)
    stats = jnp.concatenate(
        [local_acc, local_sum[..., None], local_top[..., None]], axis=-1
    )
    stats = butterfly(stats, softmax_merge, ["z", "core", "x"])
    mixture = stats[..., :HDIM]
    totals = stats[..., HDIM]
    mixed = (mixture / totals[..., None]).astype(jnp.bfloat16)
    mixed_rows = mixed.reshape(requests, feat_width)
    out_terms = jnp.dot(mixed_rows, w_out, preferred_element_type=jnp.float32)
    attn_out = butterfly(out_terms, jnp.add, ["heads"]).astype(jnp.bfloat16)
    return (packed_keys, packed_values, packed_request, folded_keys, folded_values, attn_out)


def solution(mesh):
    heads_count, seq_count = mesh.devices.shape
    fine = Mesh(
        mesh.devices.reshape(heads_count, seq_count // 8, 4, 2),
        ("heads",) + SEQ_PARTS,
    )
    seq = SEQ_PARTS
    return jax.shard_map(
        shards,
        mesh=fine,
        in_specs=(
            P(None, seq),
            P(seq, None, "heads"),
            P("heads", seq),
            P(),
            P(),
            P(seq),
            P(seq),
            P(seq, None, "heads"),
            P(seq, None, "heads"),
            P(seq, None),
        ),
        out_specs=(
            P(seq, None, "heads"),
            P(seq, None, "heads"),
            P(seq),
            P(seq, "heads"),
            P(seq, "heads"),
            P(None, seq),
        ),
        check_vma=False,
    )
```

```python
import math

import jax
import jax.numpy as jnp
from jax import lax
from jax.sharding import Mesh
from jax.sharding import PartitionSpec as P

D = 2048
HDIM = 64
ROWS = 128
HOPS = 4
CAP = 4
SLOT_DEV = 16


ROPE_BASE = 130000.0
NORM_EPSILON = 1e-05
MASKED_SCORE = -1e30

SEQ_PARTS = ("z", "x", "core")


AXIS_SIZES = {"heads": 4, "z": 8, "x": 4, "core": 2}


def exchange_steps(axes):
    for axis in axes:
        bit = 1
        while bit < AXIS_SIZES[axis]:
            yield axis, [(i, i ^ bit) for i in range(AXIS_SIZES[axis])]
            bit *= 2


def butterfly(x, merge, axes):
    for axis, pairs in exchange_steps(axes):
        x = merge(x, lax.ppermute(x, axis, pairs))
    return x


def seq_sum(x):
    return butterfly(x, jnp.add, reversed(SEQ_PARTS))


def softmax_merge(mine, theirs):
    top_a, top_b = mine[..., -1:], theirs[..., -1:]
    top = jnp.maximum(top_a, top_b)
    scale_a = jnp.exp(top_a - top)
    scale_b = jnp.exp(top_b - top)
    merged = mine[..., :-1] * scale_a + theirs[..., :-1] * scale_b
    return jnp.concatenate([merged, top], axis=-1)


def seq_index():
    index = lax.axis_index(SEQ_PARTS[0])
    for axis in SEQ_PARTS[1:]:
        index = index * lax.axis_size(axis) + lax.axis_index(axis)
    return index


def seq_size():
    count = 1
    for axis in SEQ_PARTS:
        count *= lax.axis_size(axis)
    return count


def passed_along(array, by):
    count = seq_size()
    return lax.ppermute(array, SEQ_PARTS, [(i, (i + by) % count) for i in range(count)])


def rotate_half(values, cos_table, sin_table):
    half = values.shape[-1] // 2
    lower = values[..., :half]
    upper = values[..., half:]
    return jnp.concatenate(
        [lower * cos_table - upper * sin_table, upper * cos_table + lower * sin_table], axis=-1
    )


def rope_tables(positions, head_size):
    half = head_size // 2
    freqs = ROPE_BASE ** (-(2.0 * jnp.arange(half, dtype=jnp.float32)) / head_size)
    angles = positions.astype(jnp.float32)[:, None] * freqs[None, :]
    return (jnp.cos(angles)[:, None, :], jnp.sin(angles)[:, None, :])


def shards(
    hidden,
    w_qkv,
    w_out,
    positions,
    req_blocks,
    keep_list,
    dest_slot,
    key_cache,
    value_cache,
    fold_weight,
):
    requests = hidden.shape[0]
    n_blocks, row_count, feat_width = key_cache.shape
    heads_here = feat_width // HDIM
    seq_count = seq_size()
    my_index = seq_index()

    widened = hidden.astype(jnp.float32)
    total_sq = seq_sum(jnp.sum(widened * widened, axis=1))
    normed = (widened * lax.rsqrt(total_sq / D + NORM_EPSILON)[:, None]).astype(jnp.bfloat16)
    partial_value = jnp.dot(
        normed, w_qkv.reshape(w_qkv.shape[0], 3 * feat_width), preferred_element_type=jnp.float32
    )
    query_sum = partial_value[:, :feat_width]
    key_values = partial_value[:, feat_width:]
    own_request = jnp.zeros((), jnp.int32)
    for axis, pairs in exchange_steps(reversed(SEQ_PARTS)):
        bit = pairs[0][1]
        upper_half = (lax.axis_index(axis) // bit) % 2 == 1
        half = key_values.shape[0] // 2
        lower, upper = key_values[:half], key_values[half:]
        kept = jnp.where(upper_half, upper, lower)
        given = jnp.where(upper_half, lower, upper)
        payload = jnp.concatenate([query_sum.reshape(-1), given.reshape(-1)])
        payload = lax.ppermute(payload, axis, pairs)
        query_sum = query_sum + payload[: query_sum.size].reshape(query_sum.shape)
        key_values = kept + payload[query_sum.size :].reshape(given.shape)
        own_request = own_request + jnp.where(upper_half, half, 0)
    cos_table, sin_table = rope_tables(positions, HDIM)
    queries = rotate_half(
        query_sum.reshape(requests, heads_here, HDIM), cos_table, sin_table
    ).astype(jnp.bfloat16)
    own_cos = lax.dynamic_index_in_dim(cos_table, own_request, keepdims=True)
    own_sin = lax.dynamic_index_in_dim(sin_table, own_request, keepdims=True)
    own_key = rotate_half(
        key_values[:, :feat_width].reshape(-1, heads_here, HDIM), own_cos[:, 0], own_sin[:, 0]
    ).astype(jnp.bfloat16)
    own_value = key_values[:, feat_width:].reshape(-1, heads_here, HDIM).astype(jnp.bfloat16)

    block_ids = jnp.arange(n_blocks, dtype=jnp.int32)
    global_ids = my_index * n_blocks + block_ids
    req_ends = jnp.cumsum(req_blocks)
    blk_req = jnp.sum((global_ids[:, None] >= req_ends[None, :]).astype(jnp.int32), axis=1)
    is_kept = keep_list == 1

    weight_sum = jnp.sum(fold_weight, axis=1)
    fold_keys = jnp.einsum(
        "bi,bif->bf",
        fold_weight,
        key_cache,
        preferred_element_type=jnp.float32,
        precision=lax.Precision.HIGHEST,
    )
    fold_values = jnp.einsum(
        "bi,bif->bf",
        fold_weight,
        value_cache,
        preferred_element_type=jnp.float32,
        precision=lax.Precision.HIGHEST,
    )
    folded_keys = jnp.where(is_kept[:, None], 0.0, fold_keys / weight_sum[:, None]).astype(
        jnp.bfloat16
    )
    folded_values = jnp.where(is_kept[:, None], 0.0, fold_values / weight_sum[:, None]).astype(
        jnp.bfloat16
    )

    owners = dest_slot // SLOT_DEV
    local_slot = dest_slot % SLOT_DEV
    hop_of = (owners - my_index) % seq_count
    earlier = (
        is_kept[None, :]
        & is_kept[:, None]
        & (hop_of[None, :] == hop_of[:, None])
        & (block_ids[None, :] < block_ids[:, None])
    )
    placed = jnp.sum(earlier.astype(jnp.int32), axis=1)
    arrivals = HOPS * CAP
    send_pos = jnp.where(is_kept, hop_of * CAP + placed, arrivals)
    targets = jnp.arange(arrivals, dtype=jnp.int32)
    hit_table = send_pos[None, :] == targets[:, None]
    has_block = jnp.any(hit_table, axis=1)
    source = jnp.sum(jnp.where(hit_table, block_ids[None, :], 0), axis=1)
    send_keys = key_cache[source].reshape(HOPS, CAP, row_count, feat_width)
    send_values = value_cache[source].reshape(HOPS, CAP, row_count, feat_width)
    meta_data = jnp.stack(
        [jnp.where(has_block, local_slot[source], -1), jnp.where(has_block, blk_req[source], -1)],
        axis=-1,
    )
    meta_data = meta_data.astype(jnp.float32).astype(jnp.bfloat16).reshape(HOPS, CAP, 2)
    arrived = [(send_keys[0], send_values[0], meta_data[0])]
    for distance in range(1, HOPS):
        arrived.append(
            passed_along((send_keys[distance], send_values[distance], meta_data[distance]), distance)
        )
    recv_keys = jnp.stack([entry[0] for entry in arrived])
    recv_values = jnp.stack([entry[1] for entry in arrived])
    recv_meta = jnp.stack([entry[2] for entry in arrived])
    recv_keys = recv_keys.reshape(arrivals, row_count, feat_width)
    recv_values = recv_values.reshape(arrivals, row_count, feat_width)
    recv_meta = recv_meta.reshape(arrivals, 2).astype(jnp.float32).astype(jnp.int32)
    match_table = recv_meta[None, :, 0] == jnp.arange(SLOT_DEV, dtype=jnp.int32)[:, None]
    filled = jnp.any(match_table, axis=1)
    picked = jnp.sum(
        jnp.where(match_table, jnp.arange(arrivals, dtype=jnp.int32)[None, :], 0), axis=1
    )
    packed_keys = jnp.where(filled[:, None, None], recv_keys[picked], jnp.zeros((), jnp.bfloat16))
    packed_values = jnp.where(
        filled[:, None, None], recv_values[picked], jnp.zeros((), jnp.bfloat16)
    )
    packed_request = jnp.where(filled, recv_meta[picked, 1], -1)

    row_req = jnp.repeat(jnp.where(is_kept, blk_req, -1), row_count)
    extra_keys = jnp.concatenate([folded_keys, own_key.reshape(-1, feat_width)], axis=0)
    extra_values = jnp.concatenate([folded_values, own_value.reshape(-1, feat_width)], axis=0)
    extra_req = jnp.concatenate(
        [jnp.where(is_kept, -1, blk_req), jnp.full((own_key.shape[0],), own_request)]
    )
    extra_bias = jnp.concatenate(
        [
            jnp.full((n_blocks,), math.log(ROWS), jnp.float32),
            jnp.zeros((own_key.shape[0],), jnp.float32),
        ]
    )
    request_ids = jnp.arange(requests, dtype=jnp.int32)[:, None]
    row_mask = (row_req[None, :] == request_ids)[:, None, :]
    extra_mask = (extra_req[None, :] == request_ids)[:, None, :]
    own_head = jnp.arange(heads_here)[:, None] == jnp.arange(heads_here)[None, :]
    spread_queries = jnp.where(
        own_head[None, :, :, None], queries[:, :, None, :], jnp.zeros((), jnp.bfloat16)
    ).reshape(requests * heads_here, feat_width)

    def scores_of(keys, mask, bias):
        raw = lax.dot_general(
            spread_queries, keys, (((1,), (1,)), ((), ())), preferred_element_type=jnp.float32
        ).reshape(requests, heads_here, -1)
        return jnp.where(mask, raw * 0.125 + bias, MASKED_SCORE)

    row_scores = scores_of(key_cache.reshape(-1, feat_width), row_mask, 0.0)
    extra_scores = scores_of(extra_keys, extra_mask, extra_bias[None, None, :])
    local_top = jnp.maximum(jnp.max(row_scores, axis=2), jnp.max(extra_scores, axis=2))
    row_expo = jnp.where(row_mask, jnp.exp(row_scores - local_top[..., None]), 0.0)
    extra_expo = jnp.where(extra_mask, jnp.exp(extra_scores - local_top[..., None]), 0.0)
    local_sum = jnp.sum(row_expo, axis=2) + jnp.sum(extra_expo, axis=2)

    def weighted_of(expo, values):
        return jnp.dot(
            expo.astype(jnp.bfloat16).reshape(requests * heads_here, -1),
            values,
            preferred_element_type=jnp.float32,
        )

    weighted = weighted_of(row_expo, value_cache.reshape(-1, feat_width)) + weighted_of(
        extra_expo, extra_values
    )
    weighted = weighted.reshape(requests, heads_here, heads_here, HDIM)
    local_acc = jnp.sum(jnp.where(own_head[None, :, :, None], weighted, 0.0), axis=2)
    stats = jnp.concatenate(
        [local_acc, local_sum[..., None], local_top[..., None]], axis=-1
    )
    stats = butterfly(stats, softmax_merge, ["z", "core"])
    recv_keys, recv_values, recv_meta, stats = lax.optimization_barrier(
        (recv_keys, recv_values, recv_meta, stats)
    )
    stats = butterfly(stats, softmax_merge, ["x"])
    mixture = stats[..., :HDIM]
    totals = stats[..., HDIM]
    mixed = (mixture / totals[..., None]).astype(jnp.bfloat16)
    mixed_rows = mixed.reshape(requests, feat_width)
    out_terms = jnp.dot(mixed_rows, w_out, preferred_element_type=jnp.float32)
    attn_out = butterfly(out_terms, jnp.add, ["heads"]).astype(jnp.bfloat16)
    return (packed_keys, packed_values, packed_request, folded_keys, folded_values, attn_out)


def solution(mesh):
    heads_count, seq_count = mesh.devices.shape
    fine = Mesh(
        mesh.devices.reshape(heads_count, seq_count // 8, 4, 2),
        ("heads",) + SEQ_PARTS,
    )
    seq = SEQ_PARTS
    return jax.shard_map(
        shards,
        mesh=fine,
        in_specs=(
            P(None, seq),
            P(seq, None, "heads"),
            P("heads", seq),
            P(),
            P(),
            P(seq),
            P(seq),
            P(seq, None, "heads"),
            P(seq, None, "heads"),
            P(seq, None),
        ),
        out_specs=(
            P(seq, None, "heads"),
            P(seq, None, "heads"),
            P(seq),
            P(seq, "heads"),
            P(seq, "heads"),
            P(None, seq),
        ),
        check_vma=False,
    )
```

```python
import math

import jax
import jax.numpy as jnp
from jax import lax
from jax.sharding import Mesh
from jax.sharding import PartitionSpec as P

D = 2048
HDIM = 64
ROWS = 128
HOPS = 4
CAP = 4
SLOT_DEV = 16


ROPE_BASE = 130000.0
NORM_EPSILON = 1e-05
MASKED_SCORE = -1e30

SEQ_PARTS = ("z", "x", "core")


AXIS_SIZES = {"heads": 4, "z": 8, "x": 4, "core": 2}


def exchange_steps(axes):
    for axis in axes:
        bit = 1
        while bit < AXIS_SIZES[axis]:
            yield axis, [(i, i ^ bit) for i in range(AXIS_SIZES[axis])]
            bit *= 2


def butterfly(x, merge, axes):
    for axis, pairs in exchange_steps(axes):
        x = merge(x, lax.ppermute(x, axis, pairs))
    return x


def seq_sum(x):
    return butterfly(x, jnp.add, reversed(SEQ_PARTS))


def softmax_merge(mine, theirs):
    top_a, top_b = mine[..., -1:], theirs[..., -1:]
    top = jnp.maximum(top_a, top_b)
    scale_a = jnp.exp(top_a - top)
    scale_b = jnp.exp(top_b - top)
    merged = mine[..., :-1] * scale_a + theirs[..., :-1] * scale_b
    return jnp.concatenate([merged, top], axis=-1)


def seq_index():
    index = lax.axis_index(SEQ_PARTS[0])
    for axis in SEQ_PARTS[1:]:
        index = index * lax.axis_size(axis) + lax.axis_index(axis)
    return index


def seq_size():
    count = 1
    for axis in SEQ_PARTS:
        count *= lax.axis_size(axis)
    return count


def passed_along(array, by):
    count = seq_size()
    return lax.ppermute(array, SEQ_PARTS, [(i, (i + by) % count) for i in range(count)])


def rotate_half(values, cos_table, sin_table):
    half = values.shape[-1] // 2
    lower = values[..., :half]
    upper = values[..., half:]
    return jnp.concatenate(
        [lower * cos_table - upper * sin_table, upper * cos_table + lower * sin_table], axis=-1
    )


def rope_tables(positions, head_size):
    half = head_size // 2
    freqs = ROPE_BASE ** (-(2.0 * jnp.arange(half, dtype=jnp.float32)) / head_size)
    angles = positions.astype(jnp.float32)[:, None] * freqs[None, :]
    return (jnp.cos(angles)[:, None, :], jnp.sin(angles)[:, None, :])


def shards(
    hidden,
    w_qkv,
    w_out,
    positions,
    req_blocks,
    keep_list,
    dest_slot,
    key_cache,
    value_cache,
    fold_weight,
):
    requests = hidden.shape[0]
    n_blocks, row_count, feat_width = key_cache.shape
    heads_here = feat_width // HDIM
    seq_count = seq_size()
    my_index = seq_index()

    widened = hidden.astype(jnp.float32)
    total_sq = seq_sum(jnp.sum(widened * widened, axis=1))
    normed = (widened * lax.rsqrt(total_sq / D + NORM_EPSILON)[:, None]).astype(jnp.bfloat16)
    partial_value = jnp.dot(
        normed, w_qkv.reshape(w_qkv.shape[0], 3 * feat_width), preferred_element_type=jnp.float32
    )
    block_ids = jnp.arange(n_blocks, dtype=jnp.int32)
    global_ids = my_index * n_blocks + block_ids
    req_ends = jnp.cumsum(req_blocks)
    blk_req = jnp.sum((global_ids[:, None] >= req_ends[None, :]).astype(jnp.int32), axis=1)
    is_kept = keep_list == 1

    weight_sum = jnp.sum(fold_weight, axis=1)
    fold_keys = jnp.einsum(
        "bi,bif->bf",
        fold_weight,
        key_cache,
        preferred_element_type=jnp.float32,
        precision=lax.Precision.HIGHEST,
    )
    fold_values = jnp.einsum(
        "bi,bif->bf",
        fold_weight,
        value_cache,
        preferred_element_type=jnp.float32,
        precision=lax.Precision.HIGHEST,
    )
    folded_keys = jnp.where(is_kept[:, None], 0.0, fold_keys / weight_sum[:, None]).astype(
        jnp.bfloat16
    )
    folded_values = jnp.where(is_kept[:, None], 0.0, fold_values / weight_sum[:, None]).astype(
        jnp.bfloat16
    )

    owners = dest_slot // SLOT_DEV
    local_slot = dest_slot % SLOT_DEV
    hop_of = (owners - my_index) % seq_count
    earlier = (
        is_kept[None, :]
        & is_kept[:, None]
        & (hop_of[None, :] == hop_of[:, None])
        & (block_ids[None, :] < block_ids[:, None])
    )
    placed = jnp.sum(earlier.astype(jnp.int32), axis=1)
    arrivals = HOPS * CAP
    send_pos = jnp.where(is_kept, hop_of * CAP + placed, arrivals)
    targets = jnp.arange(arrivals, dtype=jnp.int32)
    hit_table = send_pos[None, :] == targets[:, None]
    has_block = jnp.any(hit_table, axis=1)
    source = jnp.sum(jnp.where(hit_table, block_ids[None, :], 0), axis=1)
    send_keys = key_cache[source].reshape(HOPS, CAP, row_count, feat_width)
    send_values = value_cache[source].reshape(HOPS, CAP, row_count, feat_width)
    meta_data = jnp.stack(
        [jnp.where(has_block, local_slot[source], -1), jnp.where(has_block, blk_req[source], -1)],
        axis=-1,
    )
    meta_data = meta_data.astype(jnp.float32).astype(jnp.bfloat16).reshape(HOPS, CAP, 2)
    send_keys, send_values, meta_data, partial_value = lax.optimization_barrier(
        (send_keys, send_values, meta_data, partial_value)
    )
    query_sum = partial_value[:, :feat_width]
    key_values = partial_value[:, feat_width:]
    own_request = jnp.zeros((), jnp.int32)
    for axis, pairs in exchange_steps(reversed(SEQ_PARTS)):
        bit = pairs[0][1]
        upper_half = (lax.axis_index(axis) // bit) % 2 == 1
        half = key_values.shape[0] // 2
        lower, upper = key_values[:half], key_values[half:]
        kept = jnp.where(upper_half, upper, lower)
        given = jnp.where(upper_half, lower, upper)
        payload = jnp.concatenate([query_sum.reshape(-1), given.reshape(-1)])
        payload = lax.ppermute(payload, axis, pairs)
        query_sum = query_sum + payload[: query_sum.size].reshape(query_sum.shape)
        key_values = kept + payload[query_sum.size :].reshape(given.shape)
        own_request = own_request + jnp.where(upper_half, half, 0)
    cos_table, sin_table = rope_tables(positions, HDIM)
    queries = rotate_half(
        query_sum.reshape(requests, heads_here, HDIM), cos_table, sin_table
    ).astype(jnp.bfloat16)
    own_cos = lax.dynamic_index_in_dim(cos_table, own_request, keepdims=True)
    own_sin = lax.dynamic_index_in_dim(sin_table, own_request, keepdims=True)
    own_key = rotate_half(
        key_values[:, :feat_width].reshape(-1, heads_here, HDIM), own_cos[:, 0], own_sin[:, 0]
    ).astype(jnp.bfloat16)
    own_value = key_values[:, feat_width:].reshape(-1, heads_here, HDIM).astype(jnp.bfloat16)

    arrived = [(send_keys[0], send_values[0], meta_data[0])]
    for distance in range(1, HOPS):
        arrived.append(
            passed_along((send_keys[distance], send_values[distance], meta_data[distance]), distance)
        )
    recv_keys = jnp.stack([entry[0] for entry in arrived])
    recv_values = jnp.stack([entry[1] for entry in arrived])
    recv_meta = jnp.stack([entry[2] for entry in arrived])
    recv_keys = recv_keys.reshape(arrivals, row_count, feat_width)
    recv_values = recv_values.reshape(arrivals, row_count, feat_width)
    recv_meta = recv_meta.reshape(arrivals, 2).astype(jnp.float32).astype(jnp.int32)
    match_table = recv_meta[None, :, 0] == jnp.arange(SLOT_DEV, dtype=jnp.int32)[:, None]
    filled = jnp.any(match_table, axis=1)
    picked = jnp.sum(
        jnp.where(match_table, jnp.arange(arrivals, dtype=jnp.int32)[None, :], 0), axis=1
    )
    packed_keys = jnp.where(filled[:, None, None], recv_keys[picked], jnp.zeros((), jnp.bfloat16))
    packed_values = jnp.where(
        filled[:, None, None], recv_values[picked], jnp.zeros((), jnp.bfloat16)
    )
    packed_request = jnp.where(filled, recv_meta[picked, 1], -1)

    row_req = jnp.repeat(jnp.where(is_kept, blk_req, -1), row_count)
    extra_keys = jnp.concatenate([folded_keys, own_key.reshape(-1, feat_width)], axis=0)
    extra_values = jnp.concatenate([folded_values, own_value.reshape(-1, feat_width)], axis=0)
    extra_req = jnp.concatenate(
        [jnp.where(is_kept, -1, blk_req), jnp.full((own_key.shape[0],), own_request)]
    )
    extra_bias = jnp.concatenate(
        [
            jnp.full((n_blocks,), math.log(ROWS), jnp.float32),
            jnp.zeros((own_key.shape[0],), jnp.float32),
        ]
    )
    request_ids = jnp.arange(requests, dtype=jnp.int32)[:, None]
    row_mask = (row_req[None, :] == request_ids)[:, None, :]
    extra_mask = (extra_req[None, :] == request_ids)[:, None, :]
    own_head = jnp.arange(heads_here)[:, None] == jnp.arange(heads_here)[None, :]
    spread_queries = jnp.where(
        own_head[None, :, :, None], queries[:, :, None, :], jnp.zeros((), jnp.bfloat16)
    ).reshape(requests * heads_here, feat_width)

    def scores_of(keys, mask, bias):
        raw = lax.dot_general(
            spread_queries, keys, (((1,), (1,)), ((), ())), preferred_element_type=jnp.float32
        ).reshape(requests, heads_here, -1)
        return jnp.where(mask, raw * 0.125 + bias, MASKED_SCORE)

    row_scores = scores_of(key_cache.reshape(-1, feat_width), row_mask, 0.0)
    extra_scores = scores_of(extra_keys, extra_mask, extra_bias[None, None, :])
    local_top = jnp.maximum(jnp.max(row_scores, axis=2), jnp.max(extra_scores, axis=2))
    row_expo = jnp.where(row_mask, jnp.exp(row_scores - local_top[..., None]), 0.0)
    extra_expo = jnp.where(extra_mask, jnp.exp(extra_scores - local_top[..., None]), 0.0)
    local_sum = jnp.sum(row_expo, axis=2) + jnp.sum(extra_expo, axis=2)

    def weighted_of(expo, values):
        return jnp.dot(
            expo.astype(jnp.bfloat16).reshape(requests * heads_here, -1),
            values,
            preferred_element_type=jnp.float32,
        )

    weighted = weighted_of(row_expo, value_cache.reshape(-1, feat_width)) + weighted_of(
        extra_expo, extra_values
    )
    weighted = weighted.reshape(requests, heads_here, heads_here, HDIM)
    local_acc = jnp.sum(jnp.where(own_head[None, :, :, None], weighted, 0.0), axis=2)
    stats = jnp.concatenate(
        [local_acc, local_sum[..., None], local_top[..., None]], axis=-1
    )
    stats = butterfly(stats, softmax_merge, ["z", "core", "x"])
    mixture = stats[..., :HDIM]
    totals = stats[..., HDIM]
    mixed = (mixture / totals[..., None]).astype(jnp.bfloat16)
    mixed_rows = mixed.reshape(requests, feat_width)
    out_terms = jnp.dot(mixed_rows, w_out, preferred_element_type=jnp.float32)
    attn_out = butterfly(out_terms, jnp.add, ["heads"]).astype(jnp.bfloat16)
    return (packed_keys, packed_values, packed_request, folded_keys, folded_values, attn_out)


def solution(mesh):
    heads_count, seq_count = mesh.devices.shape
    fine = Mesh(
        mesh.devices.reshape(heads_count, seq_count // 8, 4, 2),
        ("heads",) + SEQ_PARTS,
    )
    seq = SEQ_PARTS
    return jax.shard_map(
        shards,
        mesh=fine,
        in_specs=(
            P(None, seq),
            P(seq, None, "heads"),
            P("heads", seq),
            P(),
            P(),
            P(seq),
            P(seq),
            P(seq, None, "heads"),
            P(seq, None, "heads"),
            P(seq, None),
        ),
        out_specs=(
            P(seq, None, "heads"),
            P(seq, None, "heads"),
            P(seq),
            P(seq, "heads"),
            P(seq, "heads"),
            P(None, seq),
        ),
        check_vma=False,
    )
```

```python
import math

import jax
import jax.numpy as jnp
from jax import lax
from jax.sharding import Mesh
from jax.sharding import PartitionSpec as P

D = 2048
HDIM = 64
ROWS = 128
HOPS = 4
CAP = 4
SLOT_DEV = 16


ROPE_BASE = 130000.0
NORM_EPSILON = 1e-05
MASKED_SCORE = -1e30

SEQ_PARTS = ("z", "x", "core")


AXIS_SIZES = {"heads": 4, "z": 8, "x": 4, "core": 2}


def exchange_steps(axes):
    for axis in axes:
        bit = 1
        while bit < AXIS_SIZES[axis]:
            yield axis, [(i, i ^ bit) for i in range(AXIS_SIZES[axis])]
            bit *= 2


def butterfly(x, merge, axes):
    for axis, pairs in exchange_steps(axes):
        x = merge(x, lax.ppermute(x, axis, pairs))
    return x


def seq_sum(x):
    return butterfly(x, jnp.add, reversed(SEQ_PARTS))


def softmax_merge(mine, theirs):
    top_a, top_b = mine[..., -1:], theirs[..., -1:]
    top = jnp.maximum(top_a, top_b)
    scale_a = jnp.exp(top_a - top)
    scale_b = jnp.exp(top_b - top)
    merged = mine[..., :-1] * scale_a + theirs[..., :-1] * scale_b
    return jnp.concatenate([merged, top], axis=-1)


def seq_index():
    index = lax.axis_index(SEQ_PARTS[0])
    for axis in SEQ_PARTS[1:]:
        index = index * lax.axis_size(axis) + lax.axis_index(axis)
    return index


def seq_size():
    count = 1
    for axis in SEQ_PARTS:
        count *= lax.axis_size(axis)
    return count


def passed_along(array, by):
    count = seq_size()
    return lax.ppermute(array, SEQ_PARTS, [(i, (i + by) % count) for i in range(count)])


def rotate_half(values, cos_table, sin_table):
    half = values.shape[-1] // 2
    lower = values[..., :half]
    upper = values[..., half:]
    return jnp.concatenate(
        [lower * cos_table - upper * sin_table, upper * cos_table + lower * sin_table], axis=-1
    )


def rope_tables(positions, head_size):
    half = head_size // 2
    freqs = ROPE_BASE ** (-(2.0 * jnp.arange(half, dtype=jnp.float32)) / head_size)
    angles = positions.astype(jnp.float32)[:, None] * freqs[None, :]
    return (jnp.cos(angles)[:, None, :], jnp.sin(angles)[:, None, :])


def shards(
    hidden,
    w_qkv,
    w_out,
    positions,
    req_blocks,
    keep_list,
    dest_slot,
    key_cache,
    value_cache,
    fold_weight,
):
    requests = hidden.shape[0]
    n_blocks, row_count, feat_width = key_cache.shape
    heads_here = feat_width // HDIM
    seq_count = seq_size()
    my_index = seq_index()

    widened = hidden.astype(jnp.float32)
    total_sq = seq_sum(jnp.sum(widened * widened, axis=1))
    normed = (widened * lax.rsqrt(total_sq / D + NORM_EPSILON)[:, None]).astype(jnp.bfloat16)
    partial_value = jnp.dot(
        normed, w_qkv.reshape(w_qkv.shape[0], 3 * feat_width), preferred_element_type=jnp.float32
    )
    block_ids = jnp.arange(n_blocks, dtype=jnp.int32)
    global_ids = my_index * n_blocks + block_ids
    req_ends = jnp.cumsum(req_blocks)
    blk_req = jnp.sum((global_ids[:, None] >= req_ends[None, :]).astype(jnp.int32), axis=1)
    is_kept = keep_list == 1

    weight_sum = jnp.sum(fold_weight, axis=1)
    fold_keys = jnp.einsum(
        "bi,bif->bf",
        fold_weight,
        key_cache,
        preferred_element_type=jnp.float32,
        precision=lax.Precision.HIGHEST,
    )
    fold_values = jnp.einsum(
        "bi,bif->bf",
        fold_weight,
        value_cache,
        preferred_element_type=jnp.float32,
        precision=lax.Precision.HIGHEST,
    )
    folded_keys = jnp.where(is_kept[:, None], 0.0, fold_keys / weight_sum[:, None]).astype(
        jnp.bfloat16
    )
    folded_values = jnp.where(is_kept[:, None], 0.0, fold_values / weight_sum[:, None]).astype(
        jnp.bfloat16
    )

    owners = dest_slot // SLOT_DEV
    local_slot = dest_slot % SLOT_DEV
    hop_of = (owners - my_index) % seq_count
    earlier = (
        is_kept[None, :]
        & is_kept[:, None]
        & (hop_of[None, :] == hop_of[:, None])
        & (block_ids[None, :] < block_ids[:, None])
    )
    placed = jnp.sum(earlier.astype(jnp.int32), axis=1)
    arrivals = HOPS * CAP
    send_pos = jnp.where(is_kept, hop_of * CAP + placed, arrivals)
    targets = jnp.arange(arrivals, dtype=jnp.int32)
    hit_table = send_pos[None, :] == targets[:, None]
    has_block = jnp.any(hit_table, axis=1)
    source = jnp.sum(jnp.where(hit_table, block_ids[None, :], 0), axis=1)
    send_keys = key_cache[source].reshape(HOPS, CAP, row_count, feat_width)
    send_values = value_cache[source].reshape(HOPS, CAP, row_count, feat_width)
    meta_data = jnp.stack(
        [jnp.where(has_block, local_slot[source], -1), jnp.where(has_block, blk_req[source], -1)],
        axis=-1,
    )
    meta_data = meta_data.astype(jnp.float32).astype(jnp.bfloat16).reshape(HOPS, CAP, 2)
    send_keys, send_values, meta_data, partial_value = lax.optimization_barrier(
        (send_keys, send_values, meta_data, partial_value)
    )
    query_sum = partial_value[:, :feat_width]
    key_values = partial_value[:, feat_width:]
    own_request = jnp.zeros((), jnp.int32)
    for axis, pairs in exchange_steps(reversed(SEQ_PARTS)):
        bit = pairs[0][1]
        upper_half = (lax.axis_index(axis) // bit) % 2 == 1
        half = key_values.shape[0] // 2
        lower, upper = key_values[:half], key_values[half:]
        kept = jnp.where(upper_half, upper, lower)
        given = jnp.where(upper_half, lower, upper)
        payload = jnp.concatenate([query_sum.reshape(-1), given.reshape(-1)])
        payload = lax.ppermute(payload, axis, pairs)
        query_sum = query_sum + payload[: query_sum.size].reshape(query_sum.shape)
        key_values = kept + payload[query_sum.size :].reshape(given.shape)
        own_request = own_request + jnp.where(upper_half, half, 0)
    cos_table, sin_table = rope_tables(positions, HDIM)
    queries = rotate_half(
        query_sum.reshape(requests, heads_here, HDIM), cos_table, sin_table
    ).astype(jnp.bfloat16)
    own_cos = lax.dynamic_index_in_dim(cos_table, own_request, keepdims=True)
    own_sin = lax.dynamic_index_in_dim(sin_table, own_request, keepdims=True)
    own_key = rotate_half(
        key_values[:, :feat_width].reshape(-1, heads_here, HDIM), own_cos[:, 0], own_sin[:, 0]
    ).astype(jnp.bfloat16)
    own_value = key_values[:, feat_width:].reshape(-1, heads_here, HDIM).astype(jnp.bfloat16)

    arrived = [(send_keys[0], send_values[0], meta_data[0])]
    for distance in range(1, HOPS):
        arrived.append(
            passed_along((send_keys[distance], send_values[distance], meta_data[distance]), distance)
        )
    recv_keys = jnp.stack([entry[0] for entry in arrived])
    recv_values = jnp.stack([entry[1] for entry in arrived])
    recv_meta = jnp.stack([entry[2] for entry in arrived])
    recv_keys = recv_keys.reshape(arrivals, row_count, feat_width)
    recv_values = recv_values.reshape(arrivals, row_count, feat_width)
    recv_meta = recv_meta.reshape(arrivals, 2).astype(jnp.float32).astype(jnp.int32)
    match_table = recv_meta[None, :, 0] == jnp.arange(SLOT_DEV, dtype=jnp.int32)[:, None]
    filled = jnp.any(match_table, axis=1)
    picked = jnp.sum(
        jnp.where(match_table, jnp.arange(arrivals, dtype=jnp.int32)[None, :], 0), axis=1
    )
    packed_keys = jnp.where(filled[:, None, None], recv_keys[picked], jnp.zeros((), jnp.bfloat16))
    packed_values = jnp.where(
        filled[:, None, None], recv_values[picked], jnp.zeros((), jnp.bfloat16)
    )
    packed_request = jnp.where(filled, recv_meta[picked, 1], -1)

    row_req = jnp.repeat(jnp.where(is_kept, blk_req, -1), row_count)
    extra_keys = jnp.concatenate([folded_keys, own_key.reshape(-1, feat_width)], axis=0)
    extra_values = jnp.concatenate([folded_values, own_value.reshape(-1, feat_width)], axis=0)
    extra_req = jnp.concatenate(
        [jnp.where(is_kept, -1, blk_req), jnp.full((own_key.shape[0],), own_request)]
    )
    extra_bias = jnp.concatenate(
        [
            jnp.full((n_blocks,), math.log(ROWS), jnp.float32),
            jnp.zeros((own_key.shape[0],), jnp.float32),
        ]
    )
    request_ids = jnp.arange(requests, dtype=jnp.int32)[:, None]
    row_mask = (row_req[None, :] == request_ids)[:, None, :]
    extra_mask = (extra_req[None, :] == request_ids)[:, None, :]
    own_head = jnp.arange(heads_here)[:, None] == jnp.arange(heads_here)[None, :]
    spread_queries = jnp.where(
        own_head[None, :, :, None], queries[:, :, None, :], jnp.zeros((), jnp.bfloat16)
    ).reshape(requests * heads_here, feat_width)

    def scores_of(keys, mask, bias):
        raw = lax.dot_general(
            spread_queries, keys, (((1,), (1,)), ((), ())), preferred_element_type=jnp.float32
        ).reshape(requests, heads_here, -1)
        return jnp.where(mask, raw * 0.125 + bias, MASKED_SCORE)

    row_scores = scores_of(key_cache.reshape(-1, feat_width), row_mask, 0.0)
    extra_scores = scores_of(extra_keys, extra_mask, extra_bias[None, None, :])
    local_top = jnp.maximum(jnp.max(row_scores, axis=2), jnp.max(extra_scores, axis=2))
    row_expo = jnp.where(row_mask, jnp.exp(row_scores - local_top[..., None]), 0.0)
    extra_expo = jnp.where(extra_mask, jnp.exp(extra_scores - local_top[..., None]), 0.0)
    local_sum = jnp.sum(row_expo, axis=2) + jnp.sum(extra_expo, axis=2)

    def weighted_of(expo, values):
        return jnp.dot(
            expo.astype(jnp.bfloat16).reshape(requests * heads_here, -1),
            values,
            preferred_element_type=jnp.float32,
        )

    weighted = weighted_of(row_expo, value_cache.reshape(-1, feat_width)) + weighted_of(
        extra_expo, extra_values
    )
    weighted = weighted.reshape(requests, heads_here, heads_here, HDIM)
    local_acc = jnp.sum(jnp.where(own_head[None, :, :, None], weighted, 0.0), axis=2)
    stats = jnp.concatenate(
        [local_acc, local_sum[..., None], local_top[..., None]], axis=-1
    )
    stats = butterfly(stats, softmax_merge, ["core", "z", "x"])
    mixture = stats[..., :HDIM]
    totals = stats[..., HDIM]
    mixed = (mixture / totals[..., None]).astype(jnp.bfloat16)
    mixed_rows = mixed.reshape(requests, feat_width)
    out_terms = jnp.dot(mixed_rows, w_out, preferred_element_type=jnp.float32)
    attn_out = butterfly(out_terms, jnp.add, ["heads"]).astype(jnp.bfloat16)
    return (packed_keys, packed_values, packed_request, folded_keys, folded_values, attn_out)


def solution(mesh):
    heads_count, seq_count = mesh.devices.shape
    fine = Mesh(
        mesh.devices.reshape(heads_count, seq_count // 8, 4, 2),
        ("heads",) + SEQ_PARTS,
    )
    seq = SEQ_PARTS
    return jax.shard_map(
        shards,
        mesh=fine,
        in_specs=(
            P(None, seq),
            P(seq, None, "heads"),
            P("heads", seq),
            P(),
            P(),
            P(seq),
            P(seq),
            P(seq, None, "heads"),
            P(seq, None, "heads"),
            P(seq, None),
        ),
        out_specs=(
            P(seq, None, "heads"),
            P(seq, None, "heads"),
            P(seq),
            P(seq, "heads"),
            P(seq, "heads"),
            P(None, seq),
        ),
        check_vma=False,
    )
```
